32 devices in a mesh: req: 4 (over y, x), head: 4 (over z), dev: 2 (over core).
Axes of the slice: x: 2, y: 2, z: 4, core: 2. Of those that a mesh axis runs over, the one named last changes fastest.
Arguments:
- tokens: bfloat16 [4, 512, 2304], P('req', 'dev')
- attn_gain: float32 [2304], replicated, may hold values from 0.1 to 1.9
- w_qkv: bfloat16 [2304, 3, 2048], P(None, None, 'head')
- w_out: bfloat16 [2048, 2304], P('head'), may hold values from -0.125 to 0.125
- moe_gain: float32 [2304], replicated, may hold values from 0.1 to 1.9
- routes: int32 [4, 512, 2], P(None, 'dev'), may hold values from 0 to 7, all different within a row; in each aligned block of 256 rows (0 to 255, 256 to 511, ..., all dimensions but the last counted through in order) at most 96 rows name the same one
- route_weight: float32 [4, 512, 2], P(None, 'dev'), may hold values from 0.2 to 1
- w_gate_up: bfloat16 [8, 2, 2304, 5760], P('head', None, None, 'req'), may hold values from -0.125 to 0.125
- w_down: bfloat16 [8, 5760, 2304], P('head', 'req'), may hold values from -0.078125 to 0.078125
- kv_cache: bfloat16 [4, 16, 128, 2, 2048], P('req', None, 'dev', None, 'head'), may hold values from -6 to 6
- lengths: int32 [4], replicated, may hold values from 1 to 2048, as said below
- block_owner: int32 [4, 16], replicated, may hold values from 0 to 3, as said below
- block_slot: int32 [4, 16], replicated, may hold values from 0 to 15, as said below
Outputs:
- layer_out: bfloat16 [4, 2, 256, 2304], P('req', 'dev', 'head')
- page_pool: bfloat16 [64, 128, 2, 2048], P('req', 'dev', None, 'head')
The draws below stay inside these ranges and needn't reach their ends.
Inputs may be any that keep to these rules, and one draw needn't show every extreme that they name: `routes`: in each aligned block of 256 rows (the rows of one device) no expert is named more than 96 times; the other loads are skewed. `lengths`: each request has a length of 1 or more tokens; some request has exactly 2048. `block_owner`: each holder holds exactly 4 pages of every request. The pairs of block_owner and block_slot are distinct over all pages of all requests.
All inputs are finite; a program needn't handle non-finite values.
Results may differ from the reference program's by a relative error of at most 0.012.
Values may be sent and summed in bfloat16 or wider, within the bound.
No kernel may reach another device: no remote copies, remote signals or barrier semaphores. Data moves between devices by JAX's collectives and lax.ppermute only.
A program may use at most 192 MiB of HBM per device.

```python
import math
import jax
import jax.numpy as jnp
import numpy as np
from jax import lax

D = 2304
FF = 5760
EXPERTS = 8
TOP = 2
HD = 64
HEADS = 32
PAGE = 128
NBLK = 16
SPAN = 512
REQS = 4
HALVES = 2
HALF = 256
CAP = 96
FF_GROUPS = 4
FINISHED = 4
OWNERS = 4
CAPB = 4
MAXLEN = 2048
POOL = 64


def draw_tokens(key, part):
    key_one = jax.random.fold_in(key, 0)
    base_draw = jax.random.normal(key_one, (REQS, SPAN, D), jnp.float32)
    return base_draw.astype(jnp.bfloat16)


def draw_w_qkv(key, part):
    key_one = jax.random.fold_in(key, 0)
    base_draw = jax.random.normal(key_one, (D, 3, HEADS * HD), jnp.float32) * D ** (-0.5)
    return base_draw.astype(jnp.bfloat16)


def draw_lengths(key, part):
    key_one, key_two = jax.random.split(jax.random.fold_in(key, 3))
    drawn = jax.random.randint(key_one, (FINISHED,), 1, MAXLEN + 1)
    chosen_one = jax.random.randint(key_two, (), 0, FINISHED)
    return jnp.where(jnp.arange(FINISHED) == chosen_one, MAXLEN, drawn).astype(jnp.int32)


def page_tables(key):
    owner_key, slot_key = jax.random.split(jax.random.fold_in(key, 17))
    orders = jax.vmap(lambda single: jax.random.permutation(single, OWNERS))(jax.random.split(owner_key, FINISHED))
    blocks = jnp.arange(NBLK)
    owners = orders[:, blocks % OWNERS]
    places = jax.vmap(lambda single: jax.random.permutation(single, NBLK))(jax.random.split(slot_key, OWNERS))
    column = jnp.arange(FINISHED)[:, None] * CAPB + (blocks // OWNERS)[None, :]
    slot_ids = places[owners, column]
    return (owners.astype(jnp.int32), slot_ids.astype(jnp.int32))


def draw_block_owner(key, part):
    return page_tables(key)[0]


def draw_block_slot(key, part):
    return page_tables(key)[1]


def shard_levels(key, dims, cuts, low, top_value):
    loudness, own = 1.0, jax.random.fold_in(key, 6)
    for position, blocks in cuts:
        draws = jnp.exp(jax.random.uniform(jax.random.fold_in(own, position), (blocks,), jnp.float32, low / len(cuts), top_value / len(cuts)))
        loudness = loudness * jnp.repeat(draws, dims[position] // blocks).reshape([-1 if axis == position else 1 for axis in range(len(dims))])
    return loudness


def deal_out(key, own, number, rows, amount, top, bound, slope):
    order = jax.random.permutation(key, amount)
    packed, usual = portions_of(amount, rows * top, bound, slope, True), portions_of(amount, rows * top, bound, slope, False)
    places = jnp.arange(amount)

    def named(sizes, offset_by):
        used = int((sizes > 0).sum())
        fixed = max(1, used // 4)
        moved = fixed + (places - fixed + offset_by * (used - fixed)) % max(1, amount - fixed)
        return jnp.zeros((amount,), jnp.int32).at[order[jnp.where(places < fixed, places, moved)]].set(jnp.asarray(sizes, jnp.int32))

    sizes = jnp.where(number % 4 == 0, named(packed, number // 4), named(usual, number - number // 4 - 1))
    mixed = jax.random.permutation(jax.random.fold_in(own, 3), amount)
    source_of, receiver = mixed[0:amount // 2 * 2:2], mixed[1:amount // 2 * 2:2]
    slack = jnp.minimum(sizes[source_of] - 1, bound - sizes[receiver]) // 2
    slack = jnp.where((source_of == order[0]) | (receiver == order[0]) | (sizes[receiver] == 0), 0, jnp.maximum(slack, 0))
    moved = jax.random.randint(jax.random.fold_in(own, 4), (amount // 2,), 0, 1 << 20) % (slack + 1)
    sizes = sizes.at[source_of].add(-moved).at[receiver].add(moved)
    labels = jnp.searchsorted(jnp.cumsum(sizes), jnp.arange(rows * top), side="right").astype(jnp.int32)
    listing = labels.reshape(top, rows).T
    listing = listing[jax.random.permutation(jax.random.fold_in(own, 1), rows)]
    offset_by = jax.random.randint(jax.random.fold_in(own, 2), (rows, 1), 0, top)
    return jnp.take_along_axis(listing, (jnp.arange(top)[None, :] + offset_by) % top, axis=1)


def portions_of(count, total, most, lean, full):
    loads = [(1 << 20) // math.isqrt(standing ** lean) + 1 for standing in range(1, count + 1)]
    largest = most if full else min(most, max(-(-total // count), total * loads[0] // sum(loads)))
    least = 1 if total - largest >= count - 1 else 0
    counts, rest = [largest] + [least] * (count - 1), total - largest - least * (count - 1)
    while rest > 0:
        candidates = [i for i in range(1, count) if counts[i] < largest] or [i for i in range(1, count) if counts[i] < most]
        pool, left = sum([loads[i] for i in candidates]), rest
        for i in candidates:
            addition = min(most - counts[i], max(1, left * loads[i] // pool), rest)
            counts[i] = counts[i] + addition
            rest = rest - addition
    return np.array(counts)


def gaussian(key, dims, scale, limit, shards=(), kind=jnp.bfloat16):
    values = scale * jax.random.normal(key, dims, jnp.float32)
    if shards:
        values = values * shard_levels(key, dims, shards, -0.22, 0.18)
    return jnp.clip(values, -limit, limit).astype(kind)


def setup_inputs(seed: int = 0) -> dict:
    key_of = jax.random.split(jax.random.key(seed), 14)
    tokens = draw_tokens(jax.random.fold_in(key_of[13], 71), 0)
    attn_gain = jnp.clip(1.0 + 0.18 * jax.random.normal(key_of[1], (D,), jnp.float32), 0.1, 1.9)
    w_qkv = draw_w_qkv(jax.random.fold_in(key_of[13], 71), 0)
    w_out = gaussian(key_of[3], (HEADS * HD, D), (HEADS * HD) ** -0.5, 0.125, ((0, 4),))
    moe_gain = jnp.clip(1.0 + 0.18 * jax.random.normal(key_of[4], (D,), jnp.float32), 0.1, 1.9)
    routes_keys = jax.random.split(jax.random.fold_in(key_of[5], 1), REQS * SPAN // HALF)
    routes_turns = jax.random.permutation(jax.random.fold_in(key_of[5], 3), REQS * SPAN // HALF)
    routes = jax.vmap(lambda own, number: deal_out(jax.random.fold_in(key_of[5], 2), own, number, HALF, EXPERTS, TOP, CAP, 2))(routes_keys, routes_turns).reshape((REQS, SPAN, TOP))
    route_weight = jnp.clip(0.2 + 0.8 * jax.random.uniform(key_of[6], (REQS, SPAN, TOP), jnp.float32) ** shard_levels(key_of[6], (REQS, SPAN, TOP), ((1, 2),), -0.2, 0.2), 0.2, 1.0)
    w_gate_up = gaussian(key_of[7], (EXPERTS, 2, D, FF), D ** -0.5, 0.125, ((0, 4), (3, 4)))
    w_down = gaussian(key_of[8], (EXPERTS, FF, D), FF ** -0.5, 0.078125, ((0, 4), (1, 4)))
    kv_cache = gaussian(key_of[9], (FINISHED, NBLK, PAGE, 2, HEADS * HD), 1.0, 6.0, ((0, 4), (2, 2), (4, 4)))
    lengths = draw_lengths(jax.random.fold_in(key_of[13], 71), 0)
    block_owner = draw_block_owner(jax.random.fold_in(key_of[13], 71), 0)
    block_slot = draw_block_slot(jax.random.fold_in(key_of[13], 71), 0)
    return dict(tokens=tokens, attn_gain=attn_gain, w_qkv=w_qkv, w_out=w_out, moe_gain=moe_gain, routes=routes, route_weight=route_weight, w_gate_up=w_gate_up, w_down=w_down, kv_cache=kv_cache, lengths=lengths, block_owner=block_owner, block_slot=block_slot)


def norm_rows(values, gain_vec):
    widened = values.astype(jnp.float32)
    inv_rms = lax.rsqrt(lax.optimization_barrier(jnp.mean(widened * widened, axis=-1, keepdims=True)) + 1e-05)
    return (widened * inv_rms * gain_vec).astype(jnp.bfloat16)

def rotate(values, positions):
    half_dim = values.shape[-1] // 2
    frequency = 10000.0 ** (-jnp.arange(half_dim, dtype=jnp.float32) / half_dim)
    angles = positions[:, None] * frequency[None, :]
    cosine = jnp.cos(angles)[:, None, :]
    sine_part = jnp.sin(angles)[:, None, :]
    front_half = values[..., :half_dim]
    back_half = values[..., half_dim:]
    return jnp.concatenate([front_half * cosine - back_half * sine_part, back_half * cosine + front_half * sine_part], axis=-1)

def slot_tables(route_ids, weights, first_expert, experts_here, capacity):
    expert_ids = first_expert + jnp.arange(experts_here, dtype=jnp.int32)
    matches = (route_ids[..., None] == expert_ids).astype(jnp.float32)
    hit_shape = matches.shape
    flat_hits = matches.reshape(hit_shape[:-3] + (hit_shape[-3] * hit_shape[-2], hit_shape[-1]))
    ranking = (jnp.cumsum(flat_hits, axis=-2) - flat_hits).reshape(hit_shape)
    places = (ranking[..., None] == jnp.arange(capacity, dtype=jnp.float32)).astype(jnp.float32) * matches[..., None]
    dispatch = lax.optimization_barrier(jnp.sum(places, axis=-3))
    combine = lax.optimization_barrier(jnp.sum(places * weights[..., None, None], axis=-3))
    return (dispatch, combine)

def reference(tokens, attn_gain, w_qkv, w_out, moe_gain, routes, route_weight, w_gate_up, w_down, kv_cache, lengths, block_owner, block_slot):

    def attend_request(request_tokens):
        normed = norm_rows(request_tokens, attn_gain)
        projected = jnp.dot(normed, w_qkv.reshape(D, 3 * HEADS * HD), preferred_element_type=jnp.float32).reshape(SPAN, 3, HEADS, HD)
        positions = jnp.arange(SPAN, dtype=jnp.int32)
        angles_at = positions.astype(jnp.float32)
        queries = rotate(projected[:, 0], angles_at).astype(jnp.bfloat16)
        key_rows = rotate(projected[:, 1], angles_at).astype(jnp.bfloat16)
        values = projected[:, 2].astype(jnp.bfloat16)
        scores = jnp.einsum('qhd,khd->hqk', queries.astype(jnp.float32), key_rows.astype(jnp.float32)) * 0.125
        allowed = positions[None, :] <= positions[:, None]
        scores = jnp.where(allowed[None], scores, -1e+30)
        row_peak = lax.optimization_barrier(jnp.max(scores, axis=-1, keepdims=True))
        exp_scores = jnp.exp(scores - row_peak)
        row_total = lax.optimization_barrier(jnp.sum(exp_scores, axis=-1))
        probs = exp_scores.astype(jnp.bfloat16)
        attended = jnp.einsum('hqk,khd->qhd', probs.astype(jnp.float32), values.astype(jnp.float32)) / jnp.transpose(row_total)[:, :, None]
        attended = attended.astype(jnp.bfloat16).reshape(SPAN, HEADS * HD)
        mixed_out = jnp.dot(attended, w_out, preferred_element_type=jnp.float32)
        return (request_tokens.astype(jnp.float32) + mixed_out).astype(jnp.bfloat16)
    residual = lax.map(attend_request, tokens)
    moe_in = norm_rows(residual, moe_gain).reshape(REQS * HALVES, HALF, D)
    block_routes = routes.reshape(REQS * HALVES, HALF, TOP)
    block_weights = route_weight.reshape(REQS * HALVES, HALF, TOP)
    group_width = FF // FF_GROUPS

    def add_expert(accum, expert_id):
        dispatch, combine = slot_tables(block_routes, block_weights, expert_id, 1, CAP)
        dispatch = dispatch[:, :, 0]
        combine = combine[:, :, 0]
        picked = jnp.einsum('stc,std->scd', dispatch, moe_in.astype(jnp.float32)).astype(jnp.bfloat16).reshape(-1, D)
        gate_part = jnp.dot(picked, w_gate_up[expert_id, 0], preferred_element_type=jnp.float32)
        up_part = jnp.dot(picked, w_gate_up[expert_id, 1], preferred_element_type=jnp.float32)
        hidden = (jax.nn.silu(gate_part) * up_part).astype(jnp.bfloat16)
        grouped = jnp.einsum('rgf,gfd->rgd', hidden.reshape(-1, FF_GROUPS, group_width).astype(jnp.float32), w_down[expert_id].reshape(FF_GROUPS, group_width, D).astype(jnp.float32))
        rounded = lax.optimization_barrier(grouped.astype(jnp.bfloat16))
        expert_out = lax.optimization_barrier(jnp.sum(rounded.astype(jnp.float32), axis=1)).reshape(-1, CAP, D)
        added = jnp.einsum('stc,scd->std', combine, expert_out, precision=lax.Precision.HIGHEST)
        return (accum + added, None)
    moe, unused = lax.scan(add_expert, jnp.zeros((REQS * HALVES, HALF, D), jnp.float32), jnp.arange(EXPERTS, dtype=jnp.int32))
    layer_out = (residual.reshape(REQS * HALVES, HALF, D).astype(jnp.float32) + moe).astype(jnp.bfloat16).reshape(REQS, HALVES, HALF, D)
    token_pos = jnp.arange(MAXLEN, dtype=jnp.int32).reshape(NBLK, PAGE)
    live = token_pos[None] < lengths[:, None, None]
    live_cache = jnp.where(live[..., None, None], kv_cache, jnp.zeros((), jnp.bfloat16))
    page_index = (block_owner * NBLK + block_slot).reshape(-1).astype(jnp.int32)
    page_pool = jnp.zeros((POOL, PAGE, 2, HEADS * HD), jnp.bfloat16).at[page_index].set(live_cache.reshape(FINISHED * NBLK, PAGE, 2, HEADS * HD))
    return (layer_out, page_pool)
```

```python
import jax
import jax.numpy as jnp
from jax import lax
from jax.sharding import PartitionSpec as P

EXPERTS = 8
HD = 64


def shifted(block, axis, distance):
    devices = range(lax.axis_size(axis))
    route = [(i - distance, i) for i in devices if i - distance in devices]
    return lax.ppermute(block, axis, route)


def norm_rows(values, gain_vec):
    widened = values.astype(jnp.float32)
    inv_rms = lax.rsqrt(jnp.mean(widened * widened, axis=-1, keepdims=True) + 1e-05)
    return (widened * inv_rms * gain_vec).astype(jnp.bfloat16)


def rotate(values, positions):
    half_dim = values.shape[-1] // 2
    frequency = 10000.0 ** (-jnp.arange(half_dim, dtype=jnp.float32) / half_dim)
    angles = positions[:, None] * frequency[None, :]
    cosine = jnp.cos(angles)[:, None, :]
    sine_part = jnp.sin(angles)[:, None, :]
    front_half = values[..., :half_dim]
    back_half = values[..., half_dim:]
    return jnp.concatenate(
        [front_half * cosine - back_half * sine_part, back_half * cosine + front_half * sine_part],
        axis=-1,
    )


def slot_tables(route_ids, weights, first_expert, experts_here, capacity):
    expert_ids = first_expert + jnp.arange(experts_here, dtype=jnp.int32)
    matches = (route_ids[..., None] == expert_ids).astype(jnp.float32)
    hit_shape = matches.shape
    flat_hits = matches.reshape(hit_shape[:-3] + (hit_shape[-3] * hit_shape[-2], hit_shape[-1]))
    ranking = (jnp.cumsum(flat_hits, axis=-2) - flat_hits).reshape(hit_shape)
    places = (ranking[..., None] == jnp.arange(capacity, dtype=jnp.float32)).astype(
        jnp.float32
    ) * matches[..., None]
    dispatch = jnp.sum(places, axis=-3)
    combine = jnp.sum(places * weights[..., None, None], axis=-3)
    return (dispatch, combine)


def body(
    tokens,
    attn_gain,
    w_qkv,
    w_out,
    moe_gain,
    routes,
    route_weight,
    w_gate_up,
    w_down,
    kv_cache,
    lengths,
    block_owner,
    block_slot,
):
    half_rows = tokens.shape[1]
    model_width = tokens.shape[2]
    dev_index = lax.axis_index("dev")
    req_index = lax.axis_index("req")
    head_index = lax.axis_index("head")
    local_cols = w_qkv.shape[2]
    head_count = local_cols // HD
    normed = norm_rows(tokens[0], attn_gain)
    projected = jnp.dot(
        normed, w_qkv.reshape(model_width, 3 * local_cols), preferred_element_type=jnp.float32
    ).reshape(half_rows, 3, head_count, HD)
    query_pos = dev_index * half_rows + jnp.arange(half_rows, dtype=jnp.int32)
    angles_at = query_pos.astype(jnp.float32)
    queries = rotate(projected[:, 0], angles_at).astype(jnp.bfloat16)
    key_rows = rotate(projected[:, 1], angles_at).astype(jnp.bfloat16)
    values = projected[:, 2].astype(jnp.bfloat16)
    earlier_keys, earlier_values = shifted((key_rows, values), "dev", 1)
    all_keys = jnp.concatenate([earlier_keys, key_rows], axis=0)
    all_values = jnp.concatenate([earlier_values, values], axis=0)
    key_pos = (dev_index - 1) * half_rows + jnp.arange(2 * half_rows, dtype=jnp.int32)
    allowed = (key_pos[None, :] <= query_pos[:, None]) & (key_pos[None, :] >= 0)
    scores = (
        jnp.einsum("qhd,khd->hqk", queries, all_keys, preferred_element_type=jnp.float32) * 0.125
    )
    scores = jnp.where(allowed[None], scores, -1e30)
    row_peak = jnp.max(scores, axis=-1, keepdims=True)
    exp_scores = jnp.exp(scores - row_peak)
    row_total = jnp.sum(exp_scores, axis=-1)
    attended = (
        jnp.einsum(
            "hqk,khd->qhd",
            exp_scores.astype(jnp.bfloat16),
            all_values,
            preferred_element_type=jnp.float32,
        )
        / jnp.transpose(row_total)[:, :, None]
    )
    attended = attended.astype(jnp.bfloat16).reshape(half_rows, local_cols)
    partial_value = jnp.dot(attended, w_out, preferred_element_type=jnp.float32)
    attn_mixed = lax.psum(partial_value.astype(jnp.bfloat16), "head").astype(jnp.float32)
    residual = (tokens[0].astype(jnp.float32) + attn_mixed).astype(jnp.bfloat16)
    moe_in = norm_rows(residual, moe_gain)
    experts_here = w_gate_up.shape[0]
    first_expert = head_index * experts_here
    top_count = routes.shape[2]
    capacity = half_rows * top_count * 3 // (2 * EXPERTS)
    all_rows_here = lax.all_gather(moe_in, "req", axis=0, tiled=True)
    sources = all_rows_here.shape[0] // half_rows
    every_dispatch, every_combine = slot_tables(
        routes, route_weight, first_expert, experts_here, capacity
    )
    picked_all = jnp.einsum(
        "stec,std->sced",
        every_dispatch.astype(jnp.bfloat16),
        all_rows_here.reshape(sources, half_rows, model_width),
        preferred_element_type=jnp.float32,
    )
    picked_all = picked_all.astype(jnp.bfloat16).reshape(
        sources * capacity, experts_here, model_width
    )
    both = jnp.einsum("ned,egdf->gnef", picked_all, w_gate_up, preferred_element_type=jnp.float32)
    hidden_all = (jax.nn.silu(both[0]) * both[1]).astype(jnp.bfloat16)
    source_count = half_rows * lax.axis_size("req") // half_rows
    down_out = jnp.einsum("nef,efd->ned", hidden_all, w_down, preferred_element_type=jnp.float32)
    down_out = down_out.astype(jnp.bfloat16).reshape(
        source_count, capacity, experts_here, model_width
    )
    expert_back = lax.psum_scatter(down_out, "req", scatter_dimension=0, tiled=True)[0]
    own_dispatch = lax.dynamic_index_in_dim(every_dispatch, req_index, 0, keepdims=False)
    own_combine = lax.dynamic_index_in_dim(every_combine, req_index, 0, keepdims=False)
    token_weights = jnp.sum(own_combine, axis=-1)
    selected = jnp.einsum(
        "tec,ced->ted",
        own_dispatch.astype(jnp.bfloat16),
        expert_back,
        preferred_element_type=jnp.float32,
    )
    moe_out = jnp.sum(token_weights[:, :, None] * selected, axis=1)
    summed = lax.psum_scatter(
        moe_out.astype(jnp.bfloat16), "head", scatter_dimension=0, tiled=True
    ).astype(jnp.float32)
    rows_out = summed.shape[0]
    kept_rows = lax.dynamic_slice_in_dim(residual, head_index * rows_out, rows_out, 0)
    layer_out = (
        (kept_rows.astype(jnp.float32) + summed)
        .astype(jnp.bfloat16)
        .reshape(1, 1, rows_out, model_width)
    )
    owners_total = lax.axis_size("req")
    block_total = block_owner.shape[1]
    finished_total = block_owner.shape[0]
    per_owner = block_total // owners_total
    block_ids = jnp.arange(block_total, dtype=jnp.int32)
    same_owner = block_owner[:, :, None] == block_owner[:, None, :]
    before_mask = block_ids[None, :] < block_ids[:, None]
    page_rank = jnp.sum((same_owner & before_mask[None]).astype(jnp.int32), axis=2)
    own_owner = lax.dynamic_index_in_dim(block_owner, req_index, 0, keepdims=False)
    own_rank = lax.dynamic_index_in_dim(page_rank, req_index, 0, keepdims=False)
    dest_place = own_owner * per_owner + own_rank
    source_block = jnp.sum(
        jnp.where(dest_place[None, :] == block_ids[:, None], block_ids[None, :], 0), axis=1
    )
    page_half = kv_cache.shape[2]
    page_size = page_half * lax.axis_size("dev")
    token_pos = (
        block_ids[:, None] * page_size
        + dev_index * page_half
        + jnp.arange(page_half, dtype=jnp.int32)[None, :]
    )
    own_length = lax.dynamic_index_in_dim(lengths, req_index, 0, keepdims=False)
    live_cache = jnp.where(
        (token_pos < own_length)[:, :, None, None], kv_cache[0], jnp.zeros((), jnp.bfloat16)
    )
    outgoing = jnp.take(live_cache, source_block, axis=0)
    received = lax.all_to_all(outgoing, "req", split_axis=0, concat_axis=0, tiled=True)
    request_ids = jnp.arange(finished_total, dtype=jnp.int32)
    arrive_place = request_ids[:, None] * per_owner + page_rank
    own_blocks = block_owner == req_index
    slot_match = own_blocks[None] & (block_slot[None] == block_ids[:, None, None])
    gather_place = jnp.sum(jnp.where(slot_match, arrive_place[None], 0), axis=(1, 2))
    page_pool = jnp.take(received, gather_place, axis=0)
    return (layer_out, page_pool)


def solution(mesh):
    return jax.shard_map(
        body,
        mesh=mesh,
        in_specs=(
            P("req", "dev", None),
            P(),
            P(None, None, "head"),
            P("head", None),
            P(),
            P(None, "dev", None),
            P(None, "dev", None),
            P("head", None, None, "req"),
            P("head", "req", None),
            P("req", None, "dev", None, "head"),
            P(),
            P(),
            P(),
        ),
        out_specs=(P("req", "dev", "head", None), P("req", "dev", None, "head")),
        check_vma=False,
    )
```

```python
import jax
import jax.numpy as jnp
from jax import lax
from jax.sharding import PartitionSpec as P

EXPERTS = 8
HD = 64


def shifted(block, axis, distance):
    devices = range(lax.axis_size(axis))
    route = [(i - distance, i) for i in devices if i - distance in devices]
    return lax.ppermute(block, axis, route)


def norm_rows(values, gain_vec):
    widened = values.astype(jnp.float32)
    inv_rms = lax.rsqrt(jnp.mean(widened * widened, axis=-1, keepdims=True) + 1e-05)
    return (widened * inv_rms * gain_vec).astype(jnp.bfloat16)


def rotate(values, positions):
    half_dim = values.shape[-1] // 2
    frequency = 10000.0 ** (-jnp.arange(half_dim, dtype=jnp.float32) / half_dim)
    angles = positions[:, None] * frequency[None, :]
    cosine = jnp.cos(angles)[:, None, :]
    sine_part = jnp.sin(angles)[:, None, :]
    front_half = values[..., :half_dim]
    back_half = values[..., half_dim:]
    return jnp.concatenate(
        [front_half * cosine - back_half * sine_part, back_half * cosine + front_half * sine_part],
        axis=-1,
    )


def slot_tables(route_ids, weights, first_expert, experts_here, capacity):
    expert_ids = first_expert + jnp.arange(experts_here, dtype=jnp.int32)
    matches = (route_ids[..., None] == expert_ids).astype(jnp.float32)
    hit_shape = matches.shape
    flat_hits = matches.reshape(hit_shape[:-3] + (hit_shape[-3] * hit_shape[-2], hit_shape[-1]))
    ranking = (jnp.cumsum(flat_hits, axis=-2) - flat_hits).reshape(hit_shape)
    places = (ranking[..., None] == jnp.arange(capacity, dtype=jnp.float32)).astype(
        jnp.float32
    ) * matches[..., None]
    dispatch = jnp.sum(places, axis=-3)
    combine = jnp.sum(places * weights[..., None, None], axis=-3)
    return (dispatch, combine)


def hand_over_pages(kv_cache, lengths, block_owner, block_slot):
    dev_index = lax.axis_index("dev")
    req_index = lax.axis_index("req")
    owners_total = lax.axis_size("req")
    block_total = block_owner.shape[1]
    finished_total = block_owner.shape[0]
    per_owner = block_total // owners_total
    block_ids = jnp.arange(block_total, dtype=jnp.int32)
    same_owner = block_owner[:, :, None] == block_owner[:, None, :]
    before_mask = block_ids[None, :] < block_ids[:, None]
    page_rank = jnp.sum((same_owner & before_mask[None]).astype(jnp.int32), axis=2)
    own_owner = lax.dynamic_index_in_dim(block_owner, req_index, 0, keepdims=False)
    own_rank = lax.dynamic_index_in_dim(page_rank, req_index, 0, keepdims=False)
    dest_place = own_owner * per_owner + own_rank
    source_block = jnp.sum(
        jnp.where(dest_place[None, :] == block_ids[:, None], block_ids[None, :], 0), axis=1
    )
    page_half = kv_cache.shape[2]
    page_size = page_half * lax.axis_size("dev")
    token_pos = (
        block_ids[:, None] * page_size
        + dev_index * page_half
        + jnp.arange(page_half, dtype=jnp.int32)[None, :]
    )
    own_length = lax.dynamic_index_in_dim(lengths, req_index, 0, keepdims=False)
    live_cache = jnp.where(
        (token_pos < own_length)[:, :, None, None], kv_cache[0], jnp.zeros((), jnp.bfloat16)
    )
    outgoing = jnp.take(live_cache, source_block, axis=0)
    received = lax.all_to_all(outgoing, "req", split_axis=0, concat_axis=0, tiled=True)
    request_ids = jnp.arange(finished_total, dtype=jnp.int32)
    arrive_place = request_ids[:, None] * per_owner + page_rank
    own_blocks = block_owner == req_index
    slot_match = own_blocks[None] & (block_slot[None] == block_ids[:, None, None])
    gather_place = jnp.sum(jnp.where(slot_match, arrive_place[None], 0), axis=(1, 2))
    page_pool = jnp.take(received, gather_place, axis=0)
    return page_pool


def body(
    tokens,
    attn_gain,
    w_qkv,
    w_out,
    moe_gain,
    routes,
    route_weight,
    w_gate_up,
    w_down,
    kv_cache,
    lengths,
    block_owner,
    block_slot,
):
    half_rows = tokens.shape[1]
    model_width = tokens.shape[2]
    dev_index = lax.axis_index("dev")
    req_index = lax.axis_index("req")
    head_index = lax.axis_index("head")
    local_cols = w_qkv.shape[2]
    head_count = local_cols // HD
    normed = norm_rows(tokens[0], attn_gain)
    projected = jnp.dot(
        normed, w_qkv.reshape(model_width, 3 * local_cols), preferred_element_type=jnp.float32
    ).reshape(half_rows, 3, head_count, HD)
    query_pos = dev_index * half_rows + jnp.arange(half_rows, dtype=jnp.int32)
    angles_at = query_pos.astype(jnp.float32)
    queries = rotate(projected[:, 0], angles_at).astype(jnp.bfloat16)
    key_rows = rotate(projected[:, 1], angles_at).astype(jnp.bfloat16)
    values = projected[:, 2].astype(jnp.bfloat16)
    earlier_keys, earlier_values = shifted((key_rows, values), "dev", 1)
    all_keys = jnp.concatenate([earlier_keys, key_rows], axis=0)
    all_values = jnp.concatenate([earlier_values, values], axis=0)
    key_pos = (dev_index - 1) * half_rows + jnp.arange(2 * half_rows, dtype=jnp.int32)
    allowed = (key_pos[None, :] <= query_pos[:, None]) & (key_pos[None, :] >= 0)
    scores = (
        jnp.einsum("qhd,khd->hqk", queries, all_keys, preferred_element_type=jnp.float32) * 0.125
    )
    scores = jnp.where(allowed[None], scores, -1e30)
    row_peak = jnp.max(scores, axis=-1, keepdims=True)
    exp_scores = jnp.exp(scores - row_peak)
    row_total = jnp.sum(exp_scores, axis=-1)
    attended = (
        jnp.einsum(
            "hqk,khd->qhd",
            exp_scores.astype(jnp.bfloat16),
            all_values,
            preferred_element_type=jnp.float32,
        )
        / jnp.transpose(row_total)[:, :, None]
    )
    attended = attended.astype(jnp.bfloat16).reshape(half_rows, local_cols)
    partial_value = jnp.dot(attended, w_out, preferred_element_type=jnp.float32)
    page_pool = hand_over_pages(kv_cache, lengths, block_owner, block_slot)
    partial_value, page_pool = lax.optimization_barrier((partial_value, page_pool))
    attn_mixed = lax.psum(partial_value.astype(jnp.bfloat16), "head").astype(jnp.float32)
    residual = (tokens[0].astype(jnp.float32) + attn_mixed).astype(jnp.bfloat16)
    moe_in = norm_rows(residual, moe_gain)
    experts_here = w_gate_up.shape[0]
    first_expert = head_index * experts_here
    top_count = routes.shape[2]
    capacity = half_rows * top_count * 3 // (2 * EXPERTS)
    all_rows_here = lax.all_gather(moe_in, "req", axis=0, tiled=True)
    sources = all_rows_here.shape[0] // half_rows
    every_dispatch, every_combine = slot_tables(
        routes, route_weight, first_expert, experts_here, capacity
    )
    picked_all = jnp.einsum(
        "stec,std->sced",
        every_dispatch.astype(jnp.bfloat16),
        all_rows_here.reshape(sources, half_rows, model_width),
        preferred_element_type=jnp.float32,
    )
    picked_all = picked_all.astype(jnp.bfloat16).reshape(
        sources * capacity, experts_here, model_width
    )
    both = jnp.einsum("ned,egdf->gnef", picked_all, w_gate_up, preferred_element_type=jnp.float32)
    hidden_all = (jax.nn.silu(both[0]) * both[1]).astype(jnp.bfloat16)
    source_count = half_rows * lax.axis_size("req") // half_rows
    down_out = jnp.einsum("nef,efd->ned", hidden_all, w_down, preferred_element_type=jnp.float32)
    down_out = down_out.astype(jnp.bfloat16).reshape(
        source_count, capacity, experts_here, model_width
    )
    expert_back = lax.psum_scatter(down_out, "req", scatter_dimension=0, tiled=True)[0]
    own_dispatch = lax.dynamic_index_in_dim(every_dispatch, req_index, 0, keepdims=False)
    own_combine = lax.dynamic_index_in_dim(every_combine, req_index, 0, keepdims=False)
    token_weights = jnp.sum(own_combine, axis=-1)
    selected = jnp.einsum(
        "tec,ced->ted",
        own_dispatch.astype(jnp.bfloat16),
        expert_back,
        preferred_element_type=jnp.float32,
    )
    moe_out = jnp.sum(token_weights[:, :, None] * selected, axis=1)
    summed = lax.psum_scatter(
        moe_out.astype(jnp.bfloat16), "head", scatter_dimension=0, tiled=True
    ).astype(jnp.float32)
    rows_out = summed.shape[0]
    kept_rows = lax.dynamic_slice_in_dim(residual, head_index * rows_out, rows_out, 0)
    layer_out = (
        (kept_rows.astype(jnp.float32) + summed)
        .astype(jnp.bfloat16)
        .reshape(1, 1, rows_out, model_width)
    )
    return (layer_out, page_pool)


def solution(mesh):
    return jax.shard_map(
        body,
        mesh=mesh,
        in_specs=(
            P("req", "dev", None),
            P(),
            P(None, None, "head"),
            P("head", None),
            P(),
            P(None, "dev", None),
            P(None, "dev", None),
            P("head", None, None, "req"),
            P("head", "req", None),
            P("req", None, "dev", None, "head"),
            P(),
            P(),
            P(),
        ),
        out_specs=(P("req", "dev", "head", None), P("req", "dev", None, "head")),
        check_vma=False,
    )
```

```python
import jax
import jax.numpy as jnp
from jax import lax
from jax.sharding import PartitionSpec as P

EXPERTS = 8
HD = 64


def shifted(block, axis, distance):
    devices = range(lax.axis_size(axis))
    route = [(i - distance, i) for i in devices if i - distance in devices]
    return lax.ppermute(block, axis, route)


def norm_rows(values, gain_vec):
    widened = values.astype(jnp.float32)
    inv_rms = lax.rsqrt(jnp.mean(widened * widened, axis=-1, keepdims=True) + 1e-05)
    return (widened * inv_rms * gain_vec).astype(jnp.bfloat16)


def rotate(values, positions):
    half_dim = values.shape[-1] // 2
    frequency = 10000.0 ** (-jnp.arange(half_dim, dtype=jnp.float32) / half_dim)
    angles = positions[:, None] * frequency[None, :]
    cosine = jnp.cos(angles)[:, None, :]
    sine_part = jnp.sin(angles)[:, None, :]
    front_half = values[..., :half_dim]
    back_half = values[..., half_dim:]
    return jnp.concatenate(
        [front_half * cosine - back_half * sine_part, back_half * cosine + front_half * sine_part],
        axis=-1,
    )


def slot_tables(route_ids, weights, first_expert, experts_here, capacity):
    expert_ids = first_expert + jnp.arange(experts_here, dtype=jnp.int32)
    matches = (route_ids[..., None] == expert_ids).astype(jnp.float32)
    hit_shape = matches.shape
    flat_hits = matches.reshape(hit_shape[:-3] + (hit_shape[-3] * hit_shape[-2], hit_shape[-1]))
    ranking = (jnp.cumsum(flat_hits, axis=-2) - flat_hits).reshape(hit_shape)
    places = (ranking[..., None] == jnp.arange(capacity, dtype=jnp.float32)).astype(
        jnp.float32
    ) * matches[..., None]
    dispatch = jnp.sum(places, axis=-3)
    combine = jnp.sum(places * weights[..., None, None], axis=-3)
    return (dispatch, combine)


def body(
    tokens,
    attn_gain,
    w_qkv,
    w_out,
    moe_gain,
    routes,
    route_weight,
    w_gate_up,
    w_down,
    kv_cache,
    lengths,
    block_owner,
    block_slot,
):
    half_rows = tokens.shape[1]
    model_width = tokens.shape[2]
    dev_index = lax.axis_index("dev")
    req_index = lax.axis_index("req")
    head_index = lax.axis_index("head")
    local_cols = w_qkv.shape[2]
    head_count = local_cols // HD
    normed = norm_rows(tokens[0], attn_gain)
    projected = jnp.dot(
        normed, w_qkv.reshape(model_width, 3 * local_cols), preferred_element_type=jnp.float32
    ).reshape(half_rows, 3, head_count, HD)
    query_pos = dev_index * half_rows + jnp.arange(half_rows, dtype=jnp.int32)
    angles_at = query_pos.astype(jnp.float32)
    queries = rotate(projected[:, 0], angles_at).astype(jnp.bfloat16)
    key_rows = rotate(projected[:, 1], angles_at).astype(jnp.bfloat16)
    values = projected[:, 2].astype(jnp.bfloat16)
    earlier_keys, earlier_values = shifted((key_rows, values), "dev", 1)
    all_keys = jnp.concatenate([earlier_keys, key_rows], axis=0)
    all_values = jnp.concatenate([earlier_values, values], axis=0)
    key_pos = (dev_index - 1) * half_rows + jnp.arange(2 * half_rows, dtype=jnp.int32)
    allowed = (key_pos[None, :] <= query_pos[:, None]) & (key_pos[None, :] >= 0)
    scores = (
        jnp.einsum("qhd,khd->hqk", queries, all_keys, preferred_element_type=jnp.float32) * 0.125
    )
    scores = jnp.where(allowed[None], scores, -1e30)
    row_peak = jnp.max(scores, axis=-1, keepdims=True)
    exp_scores = jnp.exp(scores - row_peak)
    row_total = jnp.sum(exp_scores, axis=-1)
    attended = (
        jnp.einsum(
            "hqk,khd->qhd",
            exp_scores.astype(jnp.bfloat16),
            all_values,
            preferred_element_type=jnp.float32,
        )
        / jnp.transpose(row_total)[:, :, None]
    )
    attended = attended.astype(jnp.bfloat16).reshape(half_rows, local_cols)
    partial_value = jnp.dot(attended, w_out, preferred_element_type=jnp.float32)
    attn_mixed = lax.psum_scatter(
        partial_value.astype(jnp.bfloat16), "head", scatter_dimension=0, tiled=True
    ).astype(jnp.float32)
    rows_out = attn_mixed.shape[0]
    own_tokens = lax.dynamic_slice_in_dim(tokens[0], head_index * rows_out, rows_out, 0)
    kept_rows = (own_tokens.astype(jnp.float32) + attn_mixed).astype(jnp.bfloat16)
    moe_in = norm_rows(kept_rows, moe_gain)
    experts_here = w_gate_up.shape[0]
    first_expert = head_index * experts_here
    top_count = routes.shape[2]
    capacity = half_rows * top_count * 3 // (2 * EXPERTS)
    all_rows_here = lax.all_gather(moe_in, ("req", "head"), axis=0, tiled=True)
    sources = all_rows_here.shape[0] // half_rows
    every_dispatch, every_combine = slot_tables(
        routes, route_weight, first_expert, experts_here, capacity
    )
    picked_all = jnp.einsum(
        "stec,std->sced",
        every_dispatch.astype(jnp.bfloat16),
        all_rows_here.reshape(sources, half_rows, model_width),
        preferred_element_type=jnp.float32,
    )
    picked_all = picked_all.astype(jnp.bfloat16).reshape(
        sources * capacity, experts_here, model_width
    )
    both = jnp.einsum("ned,egdf->gnef", picked_all, w_gate_up, preferred_element_type=jnp.float32)
    hidden_all = (jax.nn.silu(both[0]) * both[1]).astype(jnp.bfloat16)
    source_count = half_rows * lax.axis_size("req") // half_rows
    down_out = jnp.einsum("nef,efd->ned", hidden_all, w_down, preferred_element_type=jnp.float32)
    down_out = down_out.astype(jnp.bfloat16).reshape(
        source_count, capacity, experts_here, model_width
    )
    expert_back = lax.psum_scatter(down_out, "req", scatter_dimension=0, tiled=True)[0]
    own_dispatch = lax.dynamic_index_in_dim(every_dispatch, req_index, 0, keepdims=False)
    own_combine = lax.dynamic_index_in_dim(every_combine, req_index, 0, keepdims=False)
    token_weights = jnp.sum(own_combine, axis=-1)
    selected = jnp.einsum(
        "tec,ced->ted",
        own_dispatch.astype(jnp.bfloat16),
        expert_back,
        preferred_element_type=jnp.float32,
    )
    moe_out = jnp.sum(token_weights[:, :, None] * selected, axis=1)
    summed = lax.psum_scatter(
        moe_out.astype(jnp.bfloat16), "head", scatter_dimension=0, tiled=True
    ).astype(jnp.float32)
    layer_out = (
        (kept_rows.astype(jnp.float32) + summed)
        .astype(jnp.bfloat16)
        .reshape(1, 1, rows_out, model_width)
    )
    owners_total = lax.axis_size("req")
    block_total = block_owner.shape[1]
    finished_total = block_owner.shape[0]
    per_owner = block_total // owners_total
    block_ids = jnp.arange(block_total, dtype=jnp.int32)
    same_owner = block_owner[:, :, None] == block_owner[:, None, :]
    before_mask = block_ids[None, :] < block_ids[:, None]
    page_rank = jnp.sum((same_owner & before_mask[None]).astype(jnp.int32), axis=2)
    own_owner = lax.dynamic_index_in_dim(block_owner, req_index, 0, keepdims=False)
    own_rank = lax.dynamic_index_in_dim(page_rank, req_index, 0, keepdims=False)
    dest_place = own_owner * per_owner + own_rank
    source_block = jnp.sum(
        jnp.where(dest_place[None, :] == block_ids[:, None], block_ids[None, :], 0), axis=1
    )
    page_half = kv_cache.shape[2]
    page_size = page_half * lax.axis_size("dev")
    token_pos = (
        block_ids[:, None] * page_size
        + dev_index * page_half
        + jnp.arange(page_half, dtype=jnp.int32)[None, :]
    )
    own_length = lax.dynamic_index_in_dim(lengths, req_index, 0, keepdims=False)
    live_cache = jnp.where(
        (token_pos < own_length)[:, :, None, None], kv_cache[0], jnp.zeros((), jnp.bfloat16)
    )
    outgoing = jnp.take(live_cache, source_block, axis=0)
    received = lax.all_to_all(outgoing, "req", split_axis=0, concat_axis=0, tiled=True)
    request_ids = jnp.arange(finished_total, dtype=jnp.int32)
    arrive_place = request_ids[:, None] * per_owner + page_rank
    own_blocks = block_owner == req_index
    slot_match = own_blocks[None] & (block_slot[None] == block_ids[:, None, None])
    gather_place = jnp.sum(jnp.where(slot_match, arrive_place[None], 0), axis=(1, 2))
    page_pool = jnp.take(received, gather_place, axis=0)
    return (layer_out, page_pool)


def solution(mesh):
    return jax.shard_map(
        body,
        mesh=mesh,
        in_specs=(
            P("req", "dev", None),
            P(),
            P(None, None, "head"),
            P("head", None),
            P(),
            P(None, "dev", None),
            P(None, "dev", None),
            P("head", None, None, "req"),
            P("head", "req", None),
            P("req", None, "dev", None, "head"),
            P(),
            P(),
            P(),
        ),
        out_specs=(P("req", "dev", "head", None), P("req", "dev", None, "head")),
        check_vma=False,
    )
```

```python
import jax
import jax.numpy as jnp
from jax import lax
from jax.sharding import PartitionSpec as P

EXPERTS = 8
HD = 64


def shifted(block, axis, distance):
    devices = range(lax.axis_size(axis))
    route = [(i - distance, i) for i in devices if i - distance in devices]
    return lax.ppermute(block, axis, route)


def norm_rows(values, gain_vec):
    widened = values.astype(jnp.float32)
    inv_rms = lax.rsqrt(jnp.mean(widened * widened, axis=-1, keepdims=True) + 1e-05)
    return (widened * inv_rms * gain_vec).astype(jnp.bfloat16)


def rotate(values, positions):
    half_dim = values.shape[-1] // 2
    frequency = 10000.0 ** (-jnp.arange(half_dim, dtype=jnp.float32) / half_dim)
    angles = positions[:, None] * frequency[None, :]
    cosine = jnp.cos(angles)[:, None, :]
    sine_part = jnp.sin(angles)[:, None, :]
    front_half = values[..., :half_dim]
    back_half = values[..., half_dim:]
    return jnp.concatenate(
        [front_half * cosine - back_half * sine_part, back_half * cosine + front_half * sine_part],
        axis=-1,
    )


def slot_tables(route_ids, weights, first_expert, experts_here, capacity):
    expert_ids = first_expert + jnp.arange(experts_here, dtype=jnp.int32)
    matches = (route_ids[..., None] == expert_ids).astype(jnp.float32)
    hit_shape = matches.shape
    flat_hits = matches.reshape(hit_shape[:-3] + (hit_shape[-3] * hit_shape[-2], hit_shape[-1]))
    ranking = (jnp.cumsum(flat_hits, axis=-2) - flat_hits).reshape(hit_shape)
    places = (ranking[..., None] == jnp.arange(capacity, dtype=jnp.float32)).astype(
        jnp.float32
    ) * matches[..., None]
    dispatch = jnp.sum(places, axis=-3)
    combine = jnp.sum(places * weights[..., None, None], axis=-3)
    return (dispatch, combine)


def body(
    tokens,
    attn_gain,
    w_qkv,
    w_out,
    moe_gain,
    routes,
    route_weight,
    w_gate_up,
    w_down,
    kv_cache,
    lengths,
    block_owner,
    block_slot,
):
    half_rows = tokens.shape[1]
    model_width = tokens.shape[2]
    dev_index = lax.axis_index("dev")
    req_index = lax.axis_index("req")
    head_index = lax.axis_index("head")
    local_cols = w_qkv.shape[2]
    head_count = local_cols // HD
    normed = norm_rows(tokens[0], attn_gain)
    projected = jnp.dot(
        normed, w_qkv.reshape(model_width, 3 * local_cols), preferred_element_type=jnp.float32
    ).reshape(half_rows, 3, head_count, HD)
    query_pos = dev_index * half_rows + jnp.arange(half_rows, dtype=jnp.int32)
    angles_at = query_pos.astype(jnp.float32)
    queries = rotate(projected[:, 0], angles_at).astype(jnp.bfloat16)
    key_rows = rotate(projected[:, 1], angles_at).astype(jnp.bfloat16)
    values = projected[:, 2].astype(jnp.bfloat16)
    earlier_keys, earlier_values = shifted((key_rows, values), "dev", 1)
    all_keys = jnp.concatenate([earlier_keys, key_rows], axis=0)
    all_values = jnp.concatenate([earlier_values, values], axis=0)
    key_pos = (dev_index - 1) * half_rows + jnp.arange(2 * half_rows, dtype=jnp.int32)
    allowed = (key_pos[None, :] <= query_pos[:, None]) & (key_pos[None, :] >= 0)
    scores = (
        jnp.einsum("qhd,khd->hqk", queries, all_keys, preferred_element_type=jnp.float32) * 0.125
    )
    scores = jnp.where(allowed[None], scores, -1e30)
    row_peak = jnp.max(scores, axis=-1, keepdims=True)
    exp_scores = jnp.exp(scores - row_peak)
    row_total = jnp.sum(exp_scores, axis=-1)
    attended = (
        jnp.einsum(
            "hqk,khd->qhd",
            exp_scores.astype(jnp.bfloat16),
            all_values,
            preferred_element_type=jnp.float32,
        )
        / jnp.transpose(row_total)[:, :, None]
    )
    attended = attended.astype(jnp.bfloat16).reshape(half_rows, local_cols)
    partial_value = jnp.dot(attended, w_out, preferred_element_type=jnp.float32)
    attn_mixed = lax.psum_scatter(
        partial_value.astype(jnp.bfloat16), "head", scatter_dimension=0, tiled=True
    ).astype(jnp.float32)
    rows_out = attn_mixed.shape[0]
    own_tokens = lax.dynamic_slice_in_dim(tokens[0], head_index * rows_out, rows_out, 0)
    kept_rows = (own_tokens.astype(jnp.float32) + attn_mixed).astype(jnp.bfloat16)
    moe_in = norm_rows(kept_rows, moe_gain)
    experts_here = w_gate_up.shape[0]
    first_expert = head_index * experts_here
    top_count = routes.shape[2]
    capacity = half_rows * top_count * 3 // (2 * EXPERTS)
    all_rows_here = lax.all_gather(moe_in, ("req", "head"), axis=0, tiled=True)
    sources = all_rows_here.shape[0] // half_rows
    every_dispatch, every_combine = slot_tables(
        routes, route_weight, first_expert, experts_here, capacity
    )
    picked_all = jnp.einsum(
        "stec,std->sced",
        every_dispatch.astype(jnp.bfloat16),
        all_rows_here.reshape(sources, half_rows, model_width),
        preferred_element_type=jnp.float32,
    )
    picked_all = picked_all.astype(jnp.bfloat16).reshape(
        sources * capacity, experts_here, model_width
    )
    source_count = half_rows * lax.axis_size("req") // half_rows
    picked_all = picked_all.reshape(source_count, capacity, experts_here, model_width)
    back_parts = []
    for expert in range(experts_here):
        rows_e = picked_all[:, :, expert].reshape(source_count * capacity, model_width)
        both = jnp.einsum(
            "nd,gdf->gnf", rows_e, w_gate_up[expert], preferred_element_type=jnp.float32
        )
        hidden_e = (jax.nn.silu(both[0]) * both[1]).astype(jnp.bfloat16)
        down_e = jnp.dot(hidden_e, w_down[expert], preferred_element_type=jnp.float32)
        down_e = down_e.astype(jnp.bfloat16).reshape(source_count, capacity, model_width)
        back_parts.append(
            lax.psum_scatter(down_e, "req", scatter_dimension=0, tiled=True)[0]
        )
    expert_back = jnp.stack(back_parts, axis=1)
    own_dispatch = lax.dynamic_index_in_dim(every_dispatch, req_index, 0, keepdims=False)
    own_combine = lax.dynamic_index_in_dim(every_combine, req_index, 0, keepdims=False)
    token_weights = jnp.sum(own_combine, axis=-1)
    selected = jnp.einsum(
        "tec,ced->ted",
        own_dispatch.astype(jnp.bfloat16),
        expert_back,
        preferred_element_type=jnp.float32,
    )
    moe_out = jnp.sum(token_weights[:, :, None] * selected, axis=1)
    summed = lax.psum_scatter(
        moe_out.astype(jnp.bfloat16), "head", scatter_dimension=0, tiled=True
    ).astype(jnp.float32)
    layer_out = (
        (kept_rows.astype(jnp.float32) + summed)
        .astype(jnp.bfloat16)
        .reshape(1, 1, rows_out, model_width)
    )
    owners_total = lax.axis_size("req")
    block_total = block_owner.shape[1]
    finished_total = block_owner.shape[0]
    per_owner = block_total // owners_total
    block_ids = jnp.arange(block_total, dtype=jnp.int32)
    same_owner = block_owner[:, :, None] == block_owner[:, None, :]
    before_mask = block_ids[None, :] < block_ids[:, None]
    page_rank = jnp.sum((same_owner & before_mask[None]).astype(jnp.int32), axis=2)
    own_owner = lax.dynamic_index_in_dim(block_owner, req_index, 0, keepdims=False)
    own_rank = lax.dynamic_index_in_dim(page_rank, req_index, 0, keepdims=False)
    dest_place = own_owner * per_owner + own_rank
    source_block = jnp.sum(
        jnp.where(dest_place[None, :] == block_ids[:, None], block_ids[None, :], 0), axis=1
    )
    page_half = kv_cache.shape[2]
    page_size = page_half * lax.axis_size("dev")
    token_pos = (
        block_ids[:, None] * page_size
        + dev_index * page_half
        + jnp.arange(page_half, dtype=jnp.int32)[None, :]
    )
    own_length = lax.dynamic_index_in_dim(lengths, req_index, 0, keepdims=False)
    live_cache = jnp.where(
        (token_pos < own_length)[:, :, None, None], kv_cache[0], jnp.zeros((), jnp.bfloat16)
    )
    outgoing = jnp.take(live_cache, source_block, axis=0)
    received = lax.all_to_all(outgoing, "req", split_axis=0, concat_axis=0, tiled=True)
    request_ids = jnp.arange(finished_total, dtype=jnp.int32)
    arrive_place = request_ids[:, None] * per_owner + page_rank
    own_blocks = block_owner == req_index
    slot_match = own_blocks[None] & (block_slot[None] == block_ids[:, None, None])
    gather_place = jnp.sum(jnp.where(slot_match, arrive_place[None], 0), axis=(1, 2))
    page_pool = jnp.take(received, gather_place, axis=0)
    return (layer_out, page_pool)


def solution(mesh):
    return jax.shard_map(
        body,
        mesh=mesh,
        in_specs=(
            P("req", "dev", None),
            P(),
            P(None, None, "head"),
            P("head", None),
            P(),
            P(None, "dev", None),
            P(None, "dev", None),
            P("head", None, None, "req"),
            P("head", "req", None),
            P("req", None, "dev", None, "head"),
            P(),
            P(),
            P(),
        ),
        out_specs=(P("req", "dev", "head", None), P("req", "dev", None, "head")),
        check_vma=False,
    )
```

```python
import jax
import jax.numpy as jnp
from jax import lax
from jax.sharding import PartitionSpec as P

EXPERTS = 8
HD = 64


def shifted(block, axis, distance):
    devices = range(lax.axis_size(axis))
    route = [(i - distance, i) for i in devices if i - distance in devices]
    return lax.ppermute(block, axis, route)


def norm_rows(values, gain_vec):
    widened = values.astype(jnp.float32)
    inv_rms = lax.rsqrt(jnp.mean(widened * widened, axis=-1, keepdims=True) + 1e-05)
    return (widened * inv_rms * gain_vec).astype(jnp.bfloat16)


def rotate(values, positions):
    half_dim = values.shape[-1] // 2
    frequency = 10000.0 ** (-jnp.arange(half_dim, dtype=jnp.float32) / half_dim)
    angles = positions[:, None] * frequency[None, :]
    cosine = jnp.cos(angles)[:, None, :]
    sine_part = jnp.sin(angles)[:, None, :]
    front_half = values[..., :half_dim]
    back_half = values[..., half_dim:]
    return jnp.concatenate(
        [front_half * cosine - back_half * sine_part, back_half * cosine + front_half * sine_part],
        axis=-1,
    )


def slot_tables(route_ids, weights, first_expert, experts_here, capacity):
    expert_ids = first_expert + jnp.arange(experts_here, dtype=jnp.int32)
    matches = (route_ids[..., None] == expert_ids).astype(jnp.float32)
    hit_shape = matches.shape
    flat_hits = matches.reshape(hit_shape[:-3] + (hit_shape[-3] * hit_shape[-2], hit_shape[-1]))
    ranking = (jnp.cumsum(flat_hits, axis=-2) - flat_hits).reshape(hit_shape)
    places = (ranking[..., None] == jnp.arange(capacity, dtype=jnp.float32)).astype(
        jnp.float32
    ) * matches[..., None]
    dispatch = jnp.sum(places, axis=-3)
    combine = jnp.sum(places * weights[..., None, None], axis=-3)
    return (dispatch, combine)


def body(
    tokens,
    attn_gain,
    w_qkv,
    w_out,
    moe_gain,
    routes,
    route_weight,
    w_gate_up,
    w_down,
    kv_cache,
    lengths,
    block_owner,
    block_slot,
):
    half_rows = tokens.shape[1]
    model_width = tokens.shape[2]
    dev_index = lax.axis_index("dev")
    req_index = lax.axis_index("req")
    head_index = lax.axis_index("head")
    local_cols = w_qkv.shape[2]
    head_count = local_cols // HD
    normed = norm_rows(tokens[0], attn_gain)
    projected = jnp.dot(
        normed, w_qkv.reshape(model_width, 3 * local_cols), preferred_element_type=jnp.float32
    ).reshape(half_rows, 3, head_count, HD)
    query_pos = dev_index * half_rows + jnp.arange(half_rows, dtype=jnp.int32)
    angles_at = query_pos.astype(jnp.float32)
    queries = rotate(projected[:, 0], angles_at).astype(jnp.bfloat16)
    key_rows = rotate(projected[:, 1], angles_at).astype(jnp.bfloat16)
    values = projected[:, 2].astype(jnp.bfloat16)
    earlier_keys, earlier_values = shifted((key_rows, values), "dev", 1)
    all_keys = jnp.concatenate([earlier_keys, key_rows], axis=0)
    all_values = jnp.concatenate([earlier_values, values], axis=0)
    key_pos = (dev_index - 1) * half_rows + jnp.arange(2 * half_rows, dtype=jnp.int32)
    allowed = (key_pos[None, :] <= query_pos[:, None]) & (key_pos[None, :] >= 0)
    scores = (
        jnp.einsum("qhd,khd->hqk", queries, all_keys, preferred_element_type=jnp.float32) * 0.125
    )
    scores = jnp.where(allowed[None], scores, -1e30)
    row_peak = jnp.max(scores, axis=-1, keepdims=True)
    exp_scores = jnp.exp(scores - row_peak)
    row_total = jnp.sum(exp_scores, axis=-1)
    attended = (
        jnp.einsum(
            "hqk,khd->qhd",
            exp_scores.astype(jnp.bfloat16),
            all_values,
            preferred_element_type=jnp.float32,
        )
        / jnp.transpose(row_total)[:, :, None]
    )
    attended = attended.astype(jnp.bfloat16).reshape(half_rows, local_cols)
    partial_value = jnp.dot(attended, w_out, preferred_element_type=jnp.float32)
    attn_mixed = lax.psum(partial_value.astype(jnp.bfloat16), "head").astype(jnp.float32)
    residual = (tokens[0].astype(jnp.float32) + attn_mixed).astype(jnp.bfloat16)
    moe_in = norm_rows(residual, moe_gain)
    experts_here = w_gate_up.shape[0]
    first_expert = head_index * experts_here
    top_count = routes.shape[2]
    capacity = half_rows * top_count * 3 // (2 * EXPERTS)
    own_routes = lax.dynamic_index_in_dim(routes, req_index, 0, keepdims=True)
    own_weights = lax.dynamic_index_in_dim(route_weight, req_index, 0, keepdims=True)
    own_dispatch, own_combine = slot_tables(
        own_routes, own_weights, first_expert, experts_here, capacity
    )
    own_dispatch = own_dispatch[0]
    own_combine = own_combine[0]
    picked_own = jnp.einsum(
        "tec,td->ced",
        own_dispatch.astype(jnp.bfloat16),
        moe_in,
        preferred_element_type=jnp.float32,
    ).astype(jnp.bfloat16)
    picked_all = lax.all_gather(picked_own, "req", axis=0, tiled=True)
    both = jnp.einsum("ned,egdf->gnef", picked_all, w_gate_up, preferred_element_type=jnp.float32)
    hidden_all = (jax.nn.silu(both[0]) * both[1]).astype(jnp.bfloat16)
    source_count = half_rows * lax.axis_size("req") // half_rows
    down_out = jnp.einsum("nef,efd->ned", hidden_all, w_down, preferred_element_type=jnp.float32)
    down_out = down_out.astype(jnp.bfloat16).reshape(
        source_count, capacity, experts_here, model_width
    )
    expert_back = lax.psum_scatter(down_out, "req", scatter_dimension=0, tiled=True)[0]
    token_weights = jnp.sum(own_combine, axis=-1)
    selected = jnp.einsum(
        "tec,ced->ted",
        own_dispatch.astype(jnp.bfloat16),
        expert_back,
        preferred_element_type=jnp.float32,
    )
    moe_out = jnp.sum(token_weights[:, :, None] * selected, axis=1)
    summed = lax.psum_scatter(
        moe_out.astype(jnp.bfloat16), "head", scatter_dimension=0, tiled=True
    ).astype(jnp.float32)
    rows_out = summed.shape[0]
    kept_rows = lax.dynamic_slice_in_dim(residual, head_index * rows_out, rows_out, 0)
    layer_out = (
        (kept_rows.astype(jnp.float32) + summed)
        .astype(jnp.bfloat16)
        .reshape(1, 1, rows_out, model_width)
    )
    owners_total = lax.axis_size("req")
    block_total = block_owner.shape[1]
    finished_total = block_owner.shape[0]
    per_owner = block_total // owners_total
    block_ids = jnp.arange(block_total, dtype=jnp.int32)
    same_owner = block_owner[:, :, None] == block_owner[:, None, :]
    before_mask = block_ids[None, :] < block_ids[:, None]
    page_rank = jnp.sum((same_owner & before_mask[None]).astype(jnp.int32), axis=2)
    own_owner = lax.dynamic_index_in_dim(block_owner, req_index, 0, keepdims=False)
    own_rank = lax.dynamic_index_in_dim(page_rank, req_index, 0, keepdims=False)
    dest_place = own_owner * per_owner + own_rank
    source_block = jnp.sum(
        jnp.where(dest_place[None, :] == block_ids[:, None], block_ids[None, :], 0), axis=1
    )
    page_half = kv_cache.shape[2]
    page_size = page_half * lax.axis_size("dev")
    token_pos = (
        block_ids[:, None] * page_size
        + dev_index * page_half
        + jnp.arange(page_half, dtype=jnp.int32)[None, :]
    )
    own_length = lax.dynamic_index_in_dim(lengths, req_index, 0, keepdims=False)
    live_cache = jnp.where(
        (token_pos < own_length)[:, :, None, None], kv_cache[0], jnp.zeros((), jnp.bfloat16)
    )
    outgoing = jnp.take(live_cache, source_block, axis=0)
    received = lax.all_to_all(outgoing, "req", split_axis=0, concat_axis=0, tiled=True)
    request_ids = jnp.arange(finished_total, dtype=jnp.int32)
    arrive_place = request_ids[:, None] * per_owner + page_rank
    own_blocks = block_owner == req_index
    slot_match = own_blocks[None] & (block_slot[None] == block_ids[:, None, None])
    gather_place = jnp.sum(jnp.where(slot_match, arrive_place[None], 0), axis=(1, 2))
    page_pool = jnp.take(received, gather_place, axis=0)
    return (layer_out, page_pool)


def solution(mesh):
    return jax.shard_map(
        body,
        mesh=mesh,
        in_specs=(
            P("req", "dev", None),
            P(),
            P(None, None, "head"),
            P("head", None),
            P(),
            P(None, "dev", None),
            P(None, "dev", None),
            P("head", None, None, "req"),
            P("head", "req", None),
            P("req", None, "dev", None, "head"),
            P(),
            P(),
            P(),
        ),
        out_specs=(P("req", "dev", "head", None), P("req", "dev", None, "head")),
        check_vma=False,
    )
```

```python
import jax
import jax.numpy as jnp
from jax import lax
from jax.sharding import PartitionSpec as P

EXPERTS = 8
HD = 64


def shifted(block, axis, distance):
    devices = range(lax.axis_size(axis))
    route = [(i - distance, i) for i in devices if i - distance in devices]
    return lax.ppermute(block, axis, route)


def norm_rows(values, gain_vec):
    widened = values.astype(jnp.float32)
    inv_rms = lax.rsqrt(jnp.mean(widened * widened, axis=-1, keepdims=True) + 1e-05)
    return (widened * inv_rms * gain_vec).astype(jnp.bfloat16)


def rotate(values, positions):
    half_dim = values.shape[-1] // 2
    frequency = 10000.0 ** (-jnp.arange(half_dim, dtype=jnp.float32) / half_dim)
    angles = positions[:, None] * frequency[None, :]
    cosine = jnp.cos(angles)[:, None, :]
    sine_part = jnp.sin(angles)[:, None, :]
    front_half = values[..., :half_dim]
    back_half = values[..., half_dim:]
    return jnp.concatenate(
        [front_half * cosine - back_half * sine_part, back_half * cosine + front_half * sine_part],
        axis=-1,
    )


def slot_tables(route_ids, weights, first_expert, experts_here, capacity):
    expert_ids = first_expert + jnp.arange(experts_here, dtype=jnp.int32)
    matches = (route_ids[..., None] == expert_ids).astype(jnp.float32)
    hit_shape = matches.shape
    flat_hits = matches.reshape(hit_shape[:-3] + (hit_shape[-3] * hit_shape[-2], hit_shape[-1]))
    ranking = (jnp.cumsum(flat_hits, axis=-2) - flat_hits).reshape(hit_shape)
    places = (ranking[..., None] == jnp.arange(capacity, dtype=jnp.float32)).astype(
        jnp.float32
    ) * matches[..., None]
    dispatch = jnp.sum(places, axis=-3)
    combine = jnp.sum(places * weights[..., None, None], axis=-3)
    return (dispatch, combine)


def body(
    tokens,
    attn_gain,
    w_qkv,
    w_out,
    moe_gain,
    routes,
    route_weight,
    w_gate_up,
    w_down,
    kv_cache,
    lengths,
    block_owner,
    block_slot,
):
    half_rows = tokens.shape[1]
    model_width = tokens.shape[2]
    dev_index = lax.axis_index("dev")
    req_index = lax.axis_index("req")
    head_index = lax.axis_index("head")
    local_cols = w_qkv.shape[2]
    head_count = local_cols // HD
    normed = norm_rows(tokens[0], attn_gain)
    projected = jnp.dot(
        normed, w_qkv.reshape(model_width, 3 * local_cols), preferred_element_type=jnp.float32
    ).reshape(half_rows, 3, head_count, HD)
    query_pos = dev_index * half_rows + jnp.arange(half_rows, dtype=jnp.int32)
    angles_at = query_pos.astype(jnp.float32)
    queries = rotate(projected[:, 0], angles_at).astype(jnp.bfloat16)
    key_rows = rotate(projected[:, 1], angles_at).astype(jnp.bfloat16)
    values = projected[:, 2].astype(jnp.bfloat16)
    earlier_keys, earlier_values = shifted((key_rows, values), "dev", 1)
    all_keys = jnp.concatenate([earlier_keys, key_rows], axis=0)
    all_values = jnp.concatenate([earlier_values, values], axis=0)
    key_pos = (dev_index - 1) * half_rows + jnp.arange(2 * half_rows, dtype=jnp.int32)
    allowed = (key_pos[None, :] <= query_pos[:, None]) & (key_pos[None, :] >= 0)
    scores = (
        jnp.einsum("qhd,khd->hqk", queries, all_keys, preferred_element_type=jnp.float32) * 0.125
    )
    scores = jnp.where(allowed[None], scores, -1e30)
    row_peak = jnp.max(scores, axis=-1, keepdims=True)
    exp_scores = jnp.exp(scores - row_peak)
    row_total = jnp.sum(exp_scores, axis=-1)
    attended = (
        jnp.einsum(
            "hqk,khd->qhd",
            exp_scores.astype(jnp.bfloat16),
            all_values,
            preferred_element_type=jnp.float32,
        )
        / jnp.transpose(row_total)[:, :, None]
    )
    attended = attended.astype(jnp.bfloat16).reshape(half_rows, local_cols)
    partial_value = jnp.dot(attended, w_out, preferred_element_type=jnp.float32)
    attn_mixed = lax.psum(partial_value.astype(jnp.bfloat16), "head").astype(jnp.float32)
    residual = (tokens[0].astype(jnp.float32) + attn_mixed).astype(jnp.bfloat16)
    moe_in = norm_rows(residual, moe_gain)
    experts_here = w_gate_up.shape[0]
    first_expert = head_index * experts_here
    top_count = routes.shape[2]
    capacity = half_rows * top_count * 3 // (2 * EXPERTS)
    own_routes = lax.dynamic_index_in_dim(routes, req_index, 0, keepdims=True)
    own_weights = lax.dynamic_index_in_dim(route_weight, req_index, 0, keepdims=True)
    own_dispatch, own_combine = slot_tables(
        own_routes, own_weights, first_expert, experts_here, capacity
    )
    own_dispatch = own_dispatch[0]
    own_combine = own_combine[0]
    picked_own = jnp.einsum(
        "tec,td->ced",
        own_dispatch.astype(jnp.bfloat16),
        moe_in,
        preferred_element_type=jnp.float32,
    ).astype(jnp.bfloat16)
    req_total = lax.axis_size("req")

    def partner_move(block, step):
        return lax.ppermute(block, "req", [(i, i ^ step) for i in range(req_total)])

    def experts_on(rows):
        groups = rows.shape[0]
        flat = rows.reshape(groups * capacity, experts_here, model_width)
        both = jnp.einsum("ned,egdf->gnef", flat, w_gate_up, preferred_element_type=jnp.float32)
        hidden = (jax.nn.silu(both[0]) * both[1]).astype(jnp.bfloat16)
        down = jnp.einsum("nef,efd->ned", hidden, w_down, preferred_element_type=jnp.float32)
        return down.astype(jnp.bfloat16).reshape(groups, capacity, experts_here, model_width)

    arrived = {0: picked_own}
    for step in range(1, req_total):
        if step == 3:
            arrived[step] = partner_move(arrived[1], 2)
        else:
            arrived[step] = partner_move(picked_own, step)
    plan = [[0], [1, 2]] + ([list(range(3, req_total))] if req_total > 3 else [])
    plan = [[k for k in group if k < req_total] for group in plan]
    returned = []
    for group in plan:
        if not group:
            continue
        outs = experts_on(jnp.stack([arrived[k] for k in group], axis=0))
        for slot_index, step in enumerate(group):
            part = outs[slot_index]
            returned.append(part if step == 0 else partner_move(part, step))
    token_weights = jnp.sum(own_combine, axis=-1)
    dispatch_bf = own_dispatch.astype(jnp.bfloat16)
    selected = sum(
        jnp.einsum("tec,ced->ted", dispatch_bf, part, preferred_element_type=jnp.float32)
        for part in returned
    )
    moe_out = jnp.sum(token_weights[:, :, None] * selected, axis=1)
    summed = lax.psum_scatter(
        moe_out.astype(jnp.bfloat16), "head", scatter_dimension=0, tiled=True
    ).astype(jnp.float32)
    rows_out = summed.shape[0]
    kept_rows = lax.dynamic_slice_in_dim(residual, head_index * rows_out, rows_out, 0)
    layer_out = (
        (kept_rows.astype(jnp.float32) + summed)
        .astype(jnp.bfloat16)
        .reshape(1, 1, rows_out, model_width)
    )
    owners_total = lax.axis_size("req")
    block_total = block_owner.shape[1]
    finished_total = block_owner.shape[0]
    per_owner = block_total // owners_total
    block_ids = jnp.arange(block_total, dtype=jnp.int32)
    same_owner = block_owner[:, :, None] == block_owner[:, None, :]
    before_mask = block_ids[None, :] < block_ids[:, None]
    page_rank = jnp.sum((same_owner & before_mask[None]).astype(jnp.int32), axis=2)
    own_owner = lax.dynamic_index_in_dim(block_owner, req_index, 0, keepdims=False)
    own_rank = lax.dynamic_index_in_dim(page_rank, req_index, 0, keepdims=False)
    dest_place = own_owner * per_owner + own_rank
    source_block = jnp.sum(
        jnp.where(dest_place[None, :] == block_ids[:, None], block_ids[None, :], 0), axis=1
    )
    page_half = kv_cache.shape[2]
    page_size = page_half * lax.axis_size("dev")
    token_pos = (
        block_ids[:, None] * page_size
        + dev_index * page_half
        + jnp.arange(page_half, dtype=jnp.int32)[None, :]
    )
    own_length = lax.dynamic_index_in_dim(lengths, req_index, 0, keepdims=False)
    live_cache = jnp.where(
        (token_pos < own_length)[:, :, None, None], kv_cache[0], jnp.zeros((), jnp.bfloat16)
    )
    outgoing = jnp.take(live_cache, source_block, axis=0)
    received = lax.all_to_all(outgoing, "req", split_axis=0, concat_axis=0, tiled=True)
    request_ids = jnp.arange(finished_total, dtype=jnp.int32)
    arrive_place = request_ids[:, None] * per_owner + page_rank
    own_blocks = block_owner == req_index
    slot_match = own_blocks[None] & (block_slot[None] == block_ids[:, None, None])
    gather_place = jnp.sum(jnp.where(slot_match, arrive_place[None], 0), axis=(1, 2))
    page_pool = jnp.take(received, gather_place, axis=0)
    return (layer_out, page_pool)


def solution(mesh):
    return jax.shard_map(
        body,
        mesh=mesh,
        in_specs=(
            P("req", "dev", None),
            P(),
            P(None, None, "head"),
            P("head", None),
            P(),
            P(None, "dev", None),
            P(None, "dev", None),
            P("head", None, None, "req"),
            P("head", "req", None),
            P("req", None, "dev", None, "head"),
            P(),
            P(),
            P(),
        ),
        out_specs=(P("req", "dev", "head", None), P("req", "dev", None, "head")),
        check_vma=False,
    )
```

```python
import jax
import jax.numpy as jnp
from jax import lax
from jax.sharding import PartitionSpec as P

EXPERTS = 8
HD = 64


def shifted(block, axis, distance):
    devices = range(lax.axis_size(axis))
    route = [(i - distance, i) for i in devices if i - distance in devices]
    return lax.ppermute(block, axis, route)


def norm_rows(values, gain_vec):
    widened = values.astype(jnp.float32)
    inv_rms = lax.rsqrt(jnp.mean(widened * widened, axis=-1, keepdims=True) + 1e-05)
    return (widened * inv_rms * gain_vec).astype(jnp.bfloat16)


def rotate(values, positions):
    half_dim = values.shape[-1] // 2
    frequency = 10000.0 ** (-jnp.arange(half_dim, dtype=jnp.float32) / half_dim)
    angles = positions[:, None] * frequency[None, :]
    cosine = jnp.cos(angles)[:, None, :]
    sine_part = jnp.sin(angles)[:, None, :]
    front_half = values[..., :half_dim]
    back_half = values[..., half_dim:]
    return jnp.concatenate(
        [front_half * cosine - back_half * sine_part, back_half * cosine + front_half * sine_part],
        axis=-1,
    )


def slot_tables(route_ids, weights, first_expert, experts_here, capacity):
    expert_ids = first_expert + jnp.arange(experts_here, dtype=jnp.int32)
    matches = (route_ids[..., None] == expert_ids).astype(jnp.float32)
    hit_shape = matches.shape
    flat_hits = matches.reshape(hit_shape[:-3] + (hit_shape[-3] * hit_shape[-2], hit_shape[-1]))
    ranking = (jnp.cumsum(flat_hits, axis=-2) - flat_hits).reshape(hit_shape)
    places = (ranking[..., None] == jnp.arange(capacity, dtype=jnp.float32)).astype(
        jnp.float32
    ) * matches[..., None]
    dispatch = jnp.sum(places, axis=-3)
    combine = jnp.sum(places * weights[..., None, None], axis=-3)
    return (dispatch, combine)


def body(
    tokens,
    attn_gain,
    w_qkv,
    w_out,
    moe_gain,
    routes,
    route_weight,
    w_gate_up,
    w_down,
    kv_cache,
    lengths,
    block_owner,
    block_slot,
):
    half_rows = tokens.shape[1]
    model_width = tokens.shape[2]
    dev_index = lax.axis_index("dev")
    req_index = lax.axis_index("req")
    head_index = lax.axis_index("head")
    local_cols = w_qkv.shape[2]
    head_count = local_cols // HD
    normed = norm_rows(tokens[0], attn_gain)
    projected = jnp.dot(
        normed, w_qkv.reshape(model_width, 3 * local_cols), preferred_element_type=jnp.float32
    ).reshape(half_rows, 3, head_count, HD)
    query_pos = dev_index * half_rows + jnp.arange(half_rows, dtype=jnp.int32)
    angles_at = query_pos.astype(jnp.float32)
    queries = rotate(projected[:, 0], angles_at).astype(jnp.bfloat16)
    key_rows = rotate(projected[:, 1], angles_at).astype(jnp.bfloat16)
    values = projected[:, 2].astype(jnp.bfloat16)
    earlier_keys, earlier_values = shifted((key_rows, values), "dev", 1)
    all_keys = jnp.concatenate([earlier_keys, key_rows], axis=0)
    all_values = jnp.concatenate([earlier_values, values], axis=0)
    key_pos = (dev_index - 1) * half_rows + jnp.arange(2 * half_rows, dtype=jnp.int32)
    allowed = (key_pos[None, :] <= query_pos[:, None]) & (key_pos[None, :] >= 0)
    scores = (
        jnp.einsum("qhd,khd->hqk", queries, all_keys, preferred_element_type=jnp.float32) * 0.125
    )
    scores = jnp.where(allowed[None], scores, -1e30)
    row_peak = jnp.max(scores, axis=-1, keepdims=True)
    exp_scores = jnp.exp(scores - row_peak)
    row_total = jnp.sum(exp_scores, axis=-1)
    attended = (
        jnp.einsum(
            "hqk,khd->qhd",
            exp_scores.astype(jnp.bfloat16),
            all_values,
            preferred_element_type=jnp.float32,
        )
        / jnp.transpose(row_total)[:, :, None]
    )
    attended = attended.astype(jnp.bfloat16).reshape(half_rows, local_cols)
    partial_value = jnp.dot(attended, w_out, preferred_element_type=jnp.float32)
    attn_mixed = lax.psum(partial_value.astype(jnp.bfloat16), "head").astype(jnp.float32)
    residual = (tokens[0].astype(jnp.float32) + attn_mixed).astype(jnp.bfloat16)
    moe_in = norm_rows(residual, moe_gain)
    experts_here = w_gate_up.shape[0]
    first_expert = head_index * experts_here
    top_count = routes.shape[2]
    capacity = half_rows * top_count * 3 // (2 * EXPERTS)
    own_routes = lax.dynamic_index_in_dim(routes, req_index, 0, keepdims=True)
    own_weights = lax.dynamic_index_in_dim(route_weight, req_index, 0, keepdims=True)
    own_dispatch, own_combine = slot_tables(
        own_routes, own_weights, first_expert, experts_here, capacity
    )
    own_dispatch = own_dispatch[0]
    own_combine = own_combine[0]
    picked_own = jnp.einsum(
        "tec,td->ced",
        own_dispatch.astype(jnp.bfloat16),
        moe_in,
        preferred_element_type=jnp.float32,
    ).astype(jnp.bfloat16)
    req_total = lax.axis_size("req")

    def partner_move(block, step):
        return lax.ppermute(block, "req", [(i, i ^ step) for i in range(req_total)])

    def experts_on(rows):
        groups = rows.shape[0]
        flat = rows.reshape(groups * capacity, experts_here, model_width)
        both = jnp.einsum("ned,egdf->gnef", flat, w_gate_up, preferred_element_type=jnp.float32)
        hidden = (jax.nn.silu(both[0]) * both[1]).astype(jnp.bfloat16)
        down = jnp.einsum("nef,efd->ned", hidden, w_down, preferred_element_type=jnp.float32)
        return down.astype(jnp.bfloat16).reshape(groups, capacity, experts_here, model_width)

    arrived = {0: picked_own}
    for step in range(1, req_total):
        if step == 3:
            arrived[step] = partner_move(arrived[1], 2)
        else:
            arrived[step] = partner_move(picked_own, step)
    plan = [[0, 1, 2]] + ([list(range(3, req_total))] if req_total > 3 else [])
    plan = [[k for k in group if k < req_total] for group in plan]
    returned = []
    for group in plan:
        if not group:
            continue
        outs = experts_on(jnp.stack([arrived[k] for k in group], axis=0))
        for slot_index, step in enumerate(group):
            part = outs[slot_index]
            returned.append(part if step == 0 else partner_move(part, step))
    token_weights = jnp.sum(own_combine, axis=-1)
    dispatch_bf = own_dispatch.astype(jnp.bfloat16)
    selected = sum(
        jnp.einsum("tec,ced->ted", dispatch_bf, part, preferred_element_type=jnp.float32)
        for part in returned
    )
    moe_out = jnp.sum(token_weights[:, :, None] * selected, axis=1)
    summed = lax.psum_scatter(
        moe_out.astype(jnp.bfloat16), "head", scatter_dimension=0, tiled=True
    ).astype(jnp.float32)
    rows_out = summed.shape[0]
    kept_rows = lax.dynamic_slice_in_dim(residual, head_index * rows_out, rows_out, 0)
    layer_out = (
        (kept_rows.astype(jnp.float32) + summed)
        .astype(jnp.bfloat16)
        .reshape(1, 1, rows_out, model_width)
    )
    owners_total = lax.axis_size("req")
    block_total = block_owner.shape[1]
    finished_total = block_owner.shape[0]
    per_owner = block_total // owners_total
    block_ids = jnp.arange(block_total, dtype=jnp.int32)
    same_owner = block_owner[:, :, None] == block_owner[:, None, :]
    before_mask = block_ids[None, :] < block_ids[:, None]
    page_rank = jnp.sum((same_owner & before_mask[None]).astype(jnp.int32), axis=2)
    own_owner = lax.dynamic_index_in_dim(block_owner, req_index, 0, keepdims=False)
    own_rank = lax.dynamic_index_in_dim(page_rank, req_index, 0, keepdims=False)
    dest_place = own_owner * per_owner + own_rank
    source_block = jnp.sum(
        jnp.where(dest_place[None, :] == block_ids[:, None], block_ids[None, :], 0), axis=1
    )
    page_half = kv_cache.shape[2]
    page_size = page_half * lax.axis_size("dev")
    token_pos = (
        block_ids[:, None] * page_size
        + dev_index * page_half
        + jnp.arange(page_half, dtype=jnp.int32)[None, :]
    )
    own_length = lax.dynamic_index_in_dim(lengths, req_index, 0, keepdims=False)
    live_cache = jnp.where(
        (token_pos < own_length)[:, :, None, None], kv_cache[0], jnp.zeros((), jnp.bfloat16)
    )
    outgoing = jnp.take(live_cache, source_block, axis=0)
    received = lax.all_to_all(outgoing, "req", split_axis=0, concat_axis=0, tiled=True)
    request_ids = jnp.arange(finished_total, dtype=jnp.int32)
    arrive_place = request_ids[:, None] * per_owner + page_rank
    own_blocks = block_owner == req_index
    slot_match = own_blocks[None] & (block_slot[None] == block_ids[:, None, None])
    gather_place = jnp.sum(jnp.where(slot_match, arrive_place[None], 0), axis=(1, 2))
    page_pool = jnp.take(received, gather_place, axis=0)
    return (layer_out, page_pool)


def solution(mesh):
    return jax.shard_map(
        body,
        mesh=mesh,
        in_specs=(
            P("req", "dev", None),
            P(),
            P(None, None, "head"),
            P("head", None),
            P(),
            P(None, "dev", None),
            P(None, "dev", None),
            P("head", None, None, "req"),
            P("head", "req", None),
            P("req", None, "dev", None, "head"),
            P(),
            P(),
            P(),
        ),
        out_specs=(P("req", "dev", "head", None), P("req", "dev", None, "head")),
        check_vma=False,
    )
```

```python
import jax
import jax.numpy as jnp
from jax import lax
from jax.sharding import PartitionSpec as P

EXPERTS = 8
HD = 64


def shifted(block, axis, distance):
    devices = range(lax.axis_size(axis))
    route = [(i - distance, i) for i in devices if i - distance in devices]
    return lax.ppermute(block, axis, route)


def norm_rows(values, gain_vec):
    widened = values.astype(jnp.float32)
    inv_rms = lax.rsqrt(jnp.mean(widened * widened, axis=-1, keepdims=True) + 1e-05)
    return (widened * inv_rms * gain_vec).astype(jnp.bfloat16)


def rotate(values, positions):
    half_dim = values.shape[-1] // 2
    frequency = 10000.0 ** (-jnp.arange(half_dim, dtype=jnp.float32) / half_dim)
    angles = positions[:, None] * frequency[None, :]
    cosine = jnp.cos(angles)[:, None, :]
    sine_part = jnp.sin(angles)[:, None, :]
    front_half = values[..., :half_dim]
    back_half = values[..., half_dim:]
    return jnp.concatenate(
        [front_half * cosine - back_half * sine_part, back_half * cosine + front_half * sine_part],
        axis=-1,
    )


def slot_tables(route_ids, weights, first_expert, experts_here, capacity):
    expert_ids = first_expert + jnp.arange(experts_here, dtype=jnp.int32)
    matches = (route_ids[..., None] == expert_ids).astype(jnp.float32)
    hit_shape = matches.shape
    flat_hits = matches.reshape(hit_shape[:-3] + (hit_shape[-3] * hit_shape[-2], hit_shape[-1]))
    ranking = (jnp.cumsum(flat_hits, axis=-2) - flat_hits).reshape(hit_shape)
    places = (ranking[..., None] == jnp.arange(capacity, dtype=jnp.float32)).astype(
        jnp.float32
    ) * matches[..., None]
    dispatch = jnp.sum(places, axis=-3)
    combine = jnp.sum(places * weights[..., None, None], axis=-3)
    return (dispatch, combine)


def body(
    tokens,
    attn_gain,
    w_qkv,
    w_out,
    moe_gain,
    routes,
    route_weight,
    w_gate_up,
    w_down,
    kv_cache,
    lengths,
    block_owner,
    block_slot,
):
    half_rows = tokens.shape[1]
    model_width = tokens.shape[2]
    dev_index = lax.axis_index("dev")
    req_index = lax.axis_index("req")
    head_index = lax.axis_index("head")
    local_cols = w_qkv.shape[2]
    head_count = local_cols // HD
    normed = norm_rows(tokens[0], attn_gain)
    projected = jnp.dot(
        normed, w_qkv.reshape(model_width, 3 * local_cols), preferred_element_type=jnp.float32
    ).reshape(half_rows, 3, head_count, HD)
    query_pos = dev_index * half_rows + jnp.arange(half_rows, dtype=jnp.int32)
    angles_at = query_pos.astype(jnp.float32)
    queries = rotate(projected[:, 0], angles_at).astype(jnp.bfloat16)
    key_rows = rotate(projected[:, 1], angles_at).astype(jnp.bfloat16)
    values = projected[:, 2].astype(jnp.bfloat16)
    earlier_keys, earlier_values = shifted((key_rows, values), "dev", 1)
    all_keys = jnp.concatenate([earlier_keys, key_rows], axis=0)
    all_values = jnp.concatenate([earlier_values, values], axis=0)
    key_pos = (dev_index - 1) * half_rows + jnp.arange(2 * half_rows, dtype=jnp.int32)
    allowed = (key_pos[None, :] <= query_pos[:, None]) & (key_pos[None, :] >= 0)
    scores = (
        jnp.einsum("qhd,khd->hqk", queries, all_keys, preferred_element_type=jnp.float32) * 0.125
    )
    scores = jnp.where(allowed[None], scores, -1e30)
    row_peak = jnp.max(scores, axis=-1, keepdims=True)
    exp_scores = jnp.exp(scores - row_peak)
    row_total = jnp.sum(exp_scores, axis=-1)
    attended = (
        jnp.einsum(
            "hqk,khd->qhd",
            exp_scores.astype(jnp.bfloat16),
            all_values,
            preferred_element_type=jnp.float32,
        )
        / jnp.transpose(row_total)[:, :, None]
    )
    attended = attended.astype(jnp.bfloat16).reshape(half_rows, local_cols)
    partial_value = jnp.dot(attended, w_out, preferred_element_type=jnp.float32)
    attn_mixed = lax.psum(partial_value.astype(jnp.bfloat16), "head").astype(jnp.float32)
    residual = (tokens[0].astype(jnp.float32) + attn_mixed).astype(jnp.bfloat16)
    moe_in = norm_rows(residual, moe_gain)
    experts_here = w_gate_up.shape[0]
    first_expert = head_index * experts_here
    top_count = routes.shape[2]
    capacity = half_rows * top_count * 3 // (2 * EXPERTS)
    own_routes = lax.dynamic_index_in_dim(routes, req_index, 0, keepdims=True)
    own_weights = lax.dynamic_index_in_dim(route_weight, req_index, 0, keepdims=True)
    own_dispatch, own_combine = slot_tables(
        own_routes, own_weights, first_expert, experts_here, capacity
    )
    own_dispatch = own_dispatch[0]
    own_combine = own_combine[0]
    picked_own = jnp.einsum(
        "tec,td->ced",
        own_dispatch.astype(jnp.bfloat16),
        moe_in,
        preferred_element_type=jnp.float32,
    ).astype(jnp.bfloat16)
    req_total = lax.axis_size("req")
    dev_total = lax.axis_size("dev")
    split = dev_total > 1 and experts_here % dev_total == 0
    per_core = experts_here // dev_total if split else experts_here
    if split:
        first_here = dev_index * per_core
        gate_up_here = lax.dynamic_slice_in_dim(w_gate_up, first_here, per_core, 0)
        down_here = lax.dynamic_slice_in_dim(w_down, first_here, per_core, 0)
        rows_here = lax.all_to_all(picked_own, "dev", split_axis=1, concat_axis=0, tiled=True)
    else:
        gate_up_here, down_here, rows_here = w_gate_up, w_down, picked_own

    def partner_move(block, step):
        return lax.ppermute(block, "req", [(i, i ^ step) for i in range(req_total)])

    def experts_on(rows):
        groups = rows.shape[0]
        flat = rows.reshape(groups * rows.shape[1], per_core, model_width)
        both = jnp.einsum("ned,egdf->gnef", flat, gate_up_here, preferred_element_type=jnp.float32)
        hidden = (jax.nn.silu(both[0]) * both[1]).astype(jnp.bfloat16)
        down = jnp.einsum("nef,efd->ned", hidden, down_here, preferred_element_type=jnp.float32)
        return down.astype(jnp.bfloat16).reshape(rows.shape)

    arrived = {0: rows_here}
    for step in range(1, req_total):
        if step == 3:
            arrived[step] = partner_move(arrived[1], 2)
        else:
            arrived[step] = partner_move(rows_here, step)
    plan = [[0], [1, 2]] + ([list(range(3, req_total))] if req_total > 3 else [])
    plan = [[k for k in group if k < req_total] for group in plan]
    returned = []
    for group in plan:
        if not group:
            continue
        outs = experts_on(jnp.stack([arrived[k] for k in group], axis=0))
        for slot_index, step in enumerate(group):
            part = outs[slot_index]
            part = part if step == 0 else partner_move(part, step)
            if split:
                part = lax.all_to_all(part, "dev", split_axis=0, concat_axis=1, tiled=True)
            returned.append(part)
    token_weights = jnp.sum(own_combine, axis=-1)
    dispatch_bf = own_dispatch.astype(jnp.bfloat16)
    selected = sum(
        jnp.einsum("tec,ced->ted", dispatch_bf, part, preferred_element_type=jnp.float32)
        for part in returned
    )
    moe_out = jnp.sum(token_weights[:, :, None] * selected, axis=1)
    summed = lax.psum_scatter(
        moe_out.astype(jnp.bfloat16), "head", scatter_dimension=0, tiled=True
    ).astype(jnp.float32)
    rows_out = summed.shape[0]
    kept_rows = lax.dynamic_slice_in_dim(residual, head_index * rows_out, rows_out, 0)
    layer_out = (
        (kept_rows.astype(jnp.float32) + summed)
        .astype(jnp.bfloat16)
        .reshape(1, 1, rows_out, model_width)
    )
    owners_total = lax.axis_size("req")
    block_total = block_owner.shape[1]
    finished_total = block_owner.shape[0]
    per_owner = block_total // owners_total
    block_ids = jnp.arange(block_total, dtype=jnp.int32)
    same_owner = block_owner[:, :, None] == block_owner[:, None, :]
    before_mask = block_ids[None, :] < block_ids[:, None]
    page_rank = jnp.sum((same_owner & before_mask[None]).astype(jnp.int32), axis=2)
    own_owner = lax.dynamic_index_in_dim(block_owner, req_index, 0, keepdims=False)
    own_rank = lax.dynamic_index_in_dim(page_rank, req_index, 0, keepdims=False)
    dest_place = own_owner * per_owner + own_rank
    source_block = jnp.sum(
        jnp.where(dest_place[None, :] == block_ids[:, None], block_ids[None, :], 0), axis=1
    )
    page_half = kv_cache.shape[2]
    page_size = page_half * lax.axis_size("dev")
    token_pos = (
        block_ids[:, None] * page_size
        + dev_index * page_half
        + jnp.arange(page_half, dtype=jnp.int32)[None, :]
    )
    own_length = lax.dynamic_index_in_dim(lengths, req_index, 0, keepdims=False)
    live_cache = jnp.where(
        (token_pos < own_length)[:, :, None, None], kv_cache[0], jnp.zeros((), jnp.bfloat16)
    )
    outgoing = jnp.take(live_cache, source_block, axis=0)
    received = lax.all_to_all(outgoing, "req", split_axis=0, concat_axis=0, tiled=True)
    request_ids = jnp.arange(finished_total, dtype=jnp.int32)
    arrive_place = request_ids[:, None] * per_owner + page_rank
    own_blocks = block_owner == req_index
    slot_match = own_blocks[None] & (block_slot[None] == block_ids[:, None, None])
    gather_place = jnp.sum(jnp.where(slot_match, arrive_place[None], 0), axis=(1, 2))
    page_pool = jnp.take(received, gather_place, axis=0)
    return (layer_out, page_pool)


def solution(mesh):
    return jax.shard_map(
        body,
        mesh=mesh,
        in_specs=(
            P("req", "dev", None),
            P(),
            P(None, None, "head"),
            P("head", None),
            P(),
            P(None, "dev", None),
            P(None, "dev", None),
            P("head", None, None, "req"),
            P("head", "req", None),
            P("req", None, "dev", None, "head"),
            P(),
            P(),
            P(),
        ),
        out_specs=(P("req", "dev", "head", None), P("req", "dev", None, "head")),
        check_vma=False,
    )
```

```python
import jax
import jax.numpy as jnp
from jax import lax
from jax.sharding import PartitionSpec as P

EXPERTS = 8
HD = 64


def shifted(block, axis, distance):
    devices = range(lax.axis_size(axis))
    route = [(i - distance, i) for i in devices if i - distance in devices]
    return lax.ppermute(block, axis, route)


def norm_rows(values, gain_vec):
    widened = values.astype(jnp.float32)
    inv_rms = lax.rsqrt(jnp.mean(widened * widened, axis=-1, keepdims=True) + 1e-05)
    return (widened * inv_rms * gain_vec).astype(jnp.bfloat16)


def rotate(values, positions):
    half_dim = values.shape[-1] // 2
    frequency = 10000.0 ** (-jnp.arange(half_dim, dtype=jnp.float32) / half_dim)
    angles = positions[:, None] * frequency[None, :]
    cosine = jnp.cos(angles)[:, None, :]
    sine_part = jnp.sin(angles)[:, None, :]
    front_half = values[..., :half_dim]
    back_half = values[..., half_dim:]
    return jnp.concatenate(
        [front_half * cosine - back_half * sine_part, back_half * cosine + front_half * sine_part],
        axis=-1,
    )


def slot_tables(route_ids, weights, first_expert, experts_here, capacity):
    expert_ids = first_expert + jnp.arange(experts_here, dtype=jnp.int32)
    matches = (route_ids[..., None] == expert_ids).astype(jnp.float32)
    hit_shape = matches.shape
    flat_hits = matches.reshape(hit_shape[:-3] + (hit_shape[-3] * hit_shape[-2], hit_shape[-1]))
    ranking = (jnp.cumsum(flat_hits, axis=-2) - flat_hits).reshape(hit_shape)
    places = (ranking[..., None] == jnp.arange(capacity, dtype=jnp.float32)).astype(
        jnp.float32
    ) * matches[..., None]
    dispatch = jnp.sum(places, axis=-3)
    combine = jnp.sum(places * weights[..., None, None], axis=-3)
    return (dispatch, combine)


def body(
    tokens,
    attn_gain,
    w_qkv,
    w_out,
    moe_gain,
    routes,
    route_weight,
    w_gate_up,
    w_down,
    kv_cache,
    lengths,
    block_owner,
    block_slot,
):
    half_rows = tokens.shape[1]
    model_width = tokens.shape[2]
    dev_index = lax.axis_index("dev")
    req_index = lax.axis_index("req")
    head_index = lax.axis_index("head")
    local_cols = w_qkv.shape[2]
    head_count = local_cols // HD
    normed = norm_rows(tokens[0], attn_gain)
    projected = jnp.dot(
        normed, w_qkv.reshape(model_width, 3 * local_cols), preferred_element_type=jnp.float32
    ).reshape(half_rows, 3, head_count, HD)
    query_pos = dev_index * half_rows + jnp.arange(half_rows, dtype=jnp.int32)
    angles_at = query_pos.astype(jnp.float32)
    queries = rotate(projected[:, 0], angles_at).astype(jnp.bfloat16)
    key_rows = rotate(projected[:, 1], angles_at).astype(jnp.bfloat16)
    values = projected[:, 2].astype(jnp.bfloat16)
    earlier_keys, earlier_values = shifted((key_rows, values), "dev", 1)
    all_keys = jnp.concatenate([earlier_keys, key_rows], axis=0)
    all_values = jnp.concatenate([earlier_values, values], axis=0)
    key_pos = (dev_index - 1) * half_rows + jnp.arange(2 * half_rows, dtype=jnp.int32)
    allowed = (key_pos[None, :] <= query_pos[:, None]) & (key_pos[None, :] >= 0)
    scores = (
        jnp.einsum("qhd,khd->hqk", queries, all_keys, preferred_element_type=jnp.float32) * 0.125
    )
    scores = jnp.where(allowed[None], scores, -1e30)
    row_peak = jnp.max(scores, axis=-1, keepdims=True)
    exp_scores = jnp.exp(scores - row_peak)
    row_total = jnp.sum(exp_scores, axis=-1)
    attended = (
        jnp.einsum(
            "hqk,khd->qhd",
            exp_scores.astype(jnp.bfloat16),
            all_values,
            preferred_element_type=jnp.float32,
        )
        / jnp.transpose(row_total)[:, :, None]
    )
    attended = attended.astype(jnp.bfloat16).reshape(half_rows, local_cols)
    partial_value = jnp.dot(attended, w_out, preferred_element_type=jnp.float32)
    attn_mixed = lax.psum(partial_value.astype(jnp.bfloat16), "head").astype(jnp.float32)
    residual = (tokens[0].astype(jnp.float32) + attn_mixed).astype(jnp.bfloat16)
    moe_in = norm_rows(residual, moe_gain)
    experts_here = w_gate_up.shape[0]
    first_expert = head_index * experts_here
    top_count = routes.shape[2]
    capacity = half_rows * top_count * 3 // (2 * EXPERTS)
    own_routes = lax.dynamic_index_in_dim(routes, req_index, 0, keepdims=True)
    own_weights = lax.dynamic_index_in_dim(route_weight, req_index, 0, keepdims=True)
    own_dispatch, own_combine = slot_tables(
        own_routes, own_weights, first_expert, experts_here, capacity
    )
    own_dispatch = own_dispatch[0]
    own_combine = own_combine[0]
    picked_own = jnp.einsum(
        "tec,td->ced",
        own_dispatch.astype(jnp.bfloat16),
        moe_in,
        preferred_element_type=jnp.float32,
    ).astype(jnp.bfloat16)
    req_total = lax.axis_size("req")
    dev_total = lax.axis_size("dev")
    split = dev_total == 2 and experts_here % 2 == 0
    per_core = experts_here // 2 if split else experts_here
    swap = [(0, 1), (1, 0)]
    if split:
        mine_first = dev_index * per_core
        other_first = (1 - dev_index) * per_core
        gate_up_here = lax.dynamic_slice_in_dim(w_gate_up, mine_first, per_core, 0)
        down_here = lax.dynamic_slice_in_dim(w_down, mine_first, per_core, 0)
        mine = lax.dynamic_slice_in_dim(picked_own, mine_first, per_core, 1)
        theirs = lax.dynamic_slice_in_dim(picked_own, other_first, per_core, 1)
        rows_here = jnp.concatenate([mine, lax.ppermute(theirs, "dev", swap)], axis=0)
    else:
        gate_up_here, down_here, rows_here = w_gate_up, w_down, picked_own

    def partner_move(block, step):
        return lax.ppermute(block, "req", [(i, i ^ step) for i in range(req_total)])

    def experts_on(rows):
        groups = rows.shape[0]
        flat = rows.reshape(groups * rows.shape[1], per_core, model_width)
        both = jnp.einsum("ned,egdf->gnef", flat, gate_up_here, preferred_element_type=jnp.float32)
        hidden = (jax.nn.silu(both[0]) * both[1]).astype(jnp.bfloat16)
        down = jnp.einsum("nef,efd->ned", hidden, down_here, preferred_element_type=jnp.float32)
        return down.astype(jnp.bfloat16).reshape(rows.shape)

    arrived = {0: rows_here}
    for step in range(1, req_total):
        if step == 3:
            arrived[step] = partner_move(arrived[1], 2)
        else:
            arrived[step] = partner_move(rows_here, step)
    plan = [[0], [1, 2]] + ([list(range(3, req_total))] if req_total > 3 else [])
    plan = [[k for k in group if k < req_total] for group in plan]
    returned = []
    for group in plan:
        if not group:
            continue
        outs = experts_on(jnp.stack([arrived[k] for k in group], axis=0))
        for slot_index, step in enumerate(group):
            part = outs[slot_index]
            returned.append(part if step == 0 else partner_move(part, step))
    token_weights = jnp.sum(own_combine, axis=-1)
    dispatch_bf = own_dispatch.astype(jnp.bfloat16)

    def pick(dispatch_part, parts):
        return sum(
            jnp.einsum("tec,ced->ted", dispatch_part, part, preferred_element_type=jnp.float32)
            for part in parts
        )

    if split:
        stacked = jnp.stack(returned, axis=0)
        kept = stacked[:, :capacity]
        came = lax.ppermute(stacked[:, capacity:], "dev", swap)
        moe_out = jnp.sum(
            lax.dynamic_slice_in_dim(token_weights, mine_first, per_core, 1)[:, :, None]
            * pick(lax.dynamic_slice_in_dim(dispatch_bf, mine_first, per_core, 1), list(kept)),
            axis=1,
        ) + jnp.sum(
            lax.dynamic_slice_in_dim(token_weights, other_first, per_core, 1)[:, :, None]
            * pick(lax.dynamic_slice_in_dim(dispatch_bf, other_first, per_core, 1), list(came)),
            axis=1,
        )
    else:
        selected = pick(dispatch_bf, returned)
        moe_out = jnp.sum(token_weights[:, :, None] * selected, axis=1)
    summed = lax.psum_scatter(
        moe_out.astype(jnp.bfloat16), "head", scatter_dimension=0, tiled=True
    ).astype(jnp.float32)
    rows_out = summed.shape[0]
    kept_rows = lax.dynamic_slice_in_dim(residual, head_index * rows_out, rows_out, 0)
    layer_out = (
        (kept_rows.astype(jnp.float32) + summed)
        .astype(jnp.bfloat16)
        .reshape(1, 1, rows_out, model_width)
    )
    owners_total = lax.axis_size("req")
    block_total = block_owner.shape[1]
    finished_total = block_owner.shape[0]
    per_owner = block_total // owners_total
    block_ids = jnp.arange(block_total, dtype=jnp.int32)
    same_owner = block_owner[:, :, None] == block_owner[:, None, :]
    before_mask = block_ids[None, :] < block_ids[:, None]
    page_rank = jnp.sum((same_owner & before_mask[None]).astype(jnp.int32), axis=2)
    own_owner = lax.dynamic_index_in_dim(block_owner, req_index, 0, keepdims=False)
    own_rank = lax.dynamic_index_in_dim(page_rank, req_index, 0, keepdims=False)
    dest_place = own_owner * per_owner + own_rank
    source_block = jnp.sum(
        jnp.where(dest_place[None, :] == block_ids[:, None], block_ids[None, :], 0), axis=1
    )
    page_half = kv_cache.shape[2]
    page_size = page_half * lax.axis_size("dev")
    token_pos = (
        block_ids[:, None] * page_size
        + dev_index * page_half
        + jnp.arange(page_half, dtype=jnp.int32)[None, :]
    )
    own_length = lax.dynamic_index_in_dim(lengths, req_index, 0, keepdims=False)
    live_cache = jnp.where(
        (token_pos < own_length)[:, :, None, None], kv_cache[0], jnp.zeros((), jnp.bfloat16)
    )
    outgoing = jnp.take(live_cache, source_block, axis=0)
    received = lax.all_to_all(outgoing, "req", split_axis=0, concat_axis=0, tiled=True)
    request_ids = jnp.arange(finished_total, dtype=jnp.int32)
    arrive_place = request_ids[:, None] * per_owner + page_rank
    own_blocks = block_owner == req_index
    slot_match = own_blocks[None] & (block_slot[None] == block_ids[:, None, None])
    gather_place = jnp.sum(jnp.where(slot_match, arrive_place[None], 0), axis=(1, 2))
    page_pool = jnp.take(received, gather_place, axis=0)
    return (layer_out, page_pool)


def solution(mesh):
    return jax.shard_map(
        body,
        mesh=mesh,
        in_specs=(
            P("req", "dev", None),
            P(),
            P(None, None, "head"),
            P("head", None),
            P(),
            P(None, "dev", None),
            P(None, "dev", None),
            P("head", None, None, "req"),
            P("head", "req", None),
            P("req", None, "dev", None, "head"),
            P(),
            P(),
            P(),
        ),
        out_specs=(P("req", "dev", "head", None), P("req", "dev", None, "head")),
        check_vma=False,
    )
```

```python
import jax
import jax.numpy as jnp
from jax import lax
from jax.sharding import PartitionSpec as P

EXPERTS = 8
HD = 64


def shifted(block, axis, distance):
    devices = range(lax.axis_size(axis))
    route = [(i - distance, i) for i in devices if i - distance in devices]
    return lax.ppermute(block, axis, route)


def norm_rows(values, gain_vec):
    widened = values.astype(jnp.float32)
    inv_rms = lax.rsqrt(jnp.mean(widened * widened, axis=-1, keepdims=True) + 1e-05)
    return (widened * inv_rms * gain_vec).astype(jnp.bfloat16)


def rotate(values, positions):
    half_dim = values.shape[-1] // 2
    frequency = 10000.0 ** (-jnp.arange(half_dim, dtype=jnp.float32) / half_dim)
    angles = positions[:, None] * frequency[None, :]
    cosine = jnp.cos(angles)[:, None, :]
    sine_part = jnp.sin(angles)[:, None, :]
    front_half = values[..., :half_dim]
    back_half = values[..., half_dim:]
    return jnp.concatenate(
        [front_half * cosine - back_half * sine_part, back_half * cosine + front_half * sine_part],
        axis=-1,
    )


def slot_tables(route_ids, weights, first_expert, experts_here, capacity):
    expert_ids = first_expert + jnp.arange(experts_here, dtype=jnp.int32)
    matches = (route_ids[..., None] == expert_ids).astype(jnp.float32)
    hit_shape = matches.shape
    flat_hits = matches.reshape(hit_shape[:-3] + (hit_shape[-3] * hit_shape[-2], hit_shape[-1]))
    ranking = (jnp.cumsum(flat_hits, axis=-2) - flat_hits).reshape(hit_shape)
    places = (ranking[..., None] == jnp.arange(capacity, dtype=jnp.float32)).astype(
        jnp.float32
    ) * matches[..., None]
    dispatch = jnp.sum(places, axis=-3)
    combine = jnp.sum(places * weights[..., None, None], axis=-3)
    return (dispatch, combine)


def body(
    tokens,
    attn_gain,
    w_qkv,
    w_out,
    moe_gain,
    routes,
    route_weight,
    w_gate_up,
    w_down,
    kv_cache,
    lengths,
    block_owner,
    block_slot,
):
    half_rows = tokens.shape[1]
    model_width = tokens.shape[2]
    dev_index = lax.axis_index("dev")
    req_index = lax.axis_index("req")
    head_index = lax.axis_index("head")
    local_cols = w_qkv.shape[2]
    head_count = local_cols // HD
    normed = norm_rows(tokens[0], attn_gain)
    projected = jnp.dot(
        normed, w_qkv.reshape(model_width, 3 * local_cols), preferred_element_type=jnp.float32
    ).reshape(half_rows, 3, head_count, HD)
    query_pos = dev_index * half_rows + jnp.arange(half_rows, dtype=jnp.int32)
    angles_at = query_pos.astype(jnp.float32)
    queries = rotate(projected[:, 0], angles_at).astype(jnp.bfloat16)
    key_rows = rotate(projected[:, 1], angles_at).astype(jnp.bfloat16)
    values = projected[:, 2].astype(jnp.bfloat16)
    earlier_keys, earlier_values = shifted((key_rows, values), "dev", 1)
    all_keys = jnp.concatenate([earlier_keys, key_rows], axis=0)
    all_values = jnp.concatenate([earlier_values, values], axis=0)
    key_pos = (dev_index - 1) * half_rows + jnp.arange(2 * half_rows, dtype=jnp.int32)
    allowed = (key_pos[None, :] <= query_pos[:, None]) & (key_pos[None, :] >= 0)
    scores = (
        jnp.einsum("qhd,khd->hqk", queries, all_keys, preferred_element_type=jnp.float32) * 0.125
    )
    scores = jnp.where(allowed[None], scores, -1e30)
    row_peak = jnp.max(scores, axis=-1, keepdims=True)
    exp_scores = jnp.exp(scores - row_peak)
    row_total = jnp.sum(exp_scores, axis=-1)
    attended = (
        jnp.einsum(
            "hqk,khd->qhd",
            exp_scores.astype(jnp.bfloat16),
            all_values,
            preferred_element_type=jnp.float32,
        )
        / jnp.transpose(row_total)[:, :, None]
    )
    attended = attended.astype(jnp.bfloat16).reshape(half_rows, local_cols)
    partial_value = jnp.dot(attended, w_out, preferred_element_type=jnp.float32)
    attn_mixed = lax.psum(partial_value.astype(jnp.bfloat16), "head").astype(jnp.float32)
    residual = (tokens[0].astype(jnp.float32) + attn_mixed).astype(jnp.bfloat16)
    moe_in = norm_rows(residual, moe_gain)
    experts_here = w_gate_up.shape[0]
    first_expert = head_index * experts_here
    top_count = routes.shape[2]
    capacity = half_rows * top_count * 3 // (2 * EXPERTS)
    own_routes = lax.dynamic_index_in_dim(routes, req_index, 0, keepdims=True)
    own_weights = lax.dynamic_index_in_dim(route_weight, req_index, 0, keepdims=True)
    own_dispatch, own_combine = slot_tables(
        own_routes, own_weights, first_expert, experts_here, capacity
    )
    own_dispatch = own_dispatch[0]
    own_combine = own_combine[0]
    picked_own = jnp.einsum(
        "tec,td->ced",
        own_dispatch.astype(jnp.bfloat16),
        moe_in,
        preferred_element_type=jnp.float32,
    ).astype(jnp.bfloat16)
    req_total = lax.axis_size("req")
    dev_total = lax.axis_size("dev")
    split = dev_total == 2 and experts_here % 2 == 0
    per_core = experts_here // 2 if split else experts_here
    swap = [(0, 1), (1, 0)]
    if split:
        mine_first = dev_index * per_core
        other_first = (1 - dev_index) * per_core
        gate_up_here = lax.dynamic_slice_in_dim(w_gate_up, mine_first, per_core, 0)
        down_here = lax.dynamic_slice_in_dim(w_down, mine_first, per_core, 0)
        mine = lax.dynamic_slice_in_dim(picked_own, mine_first, per_core, 1)
        theirs = lax.dynamic_slice_in_dim(picked_own, other_first, per_core, 1)
        rows_here = jnp.concatenate([mine, lax.ppermute(theirs, "dev", swap)], axis=0)
    else:
        gate_up_here, down_here, rows_here = w_gate_up, w_down, picked_own

    def partner_move(block, step):
        return lax.ppermute(block, "req", [(i, i ^ step) for i in range(req_total)])

    def experts_on(rows):
        groups = rows.shape[0]
        flat = rows.reshape(groups * rows.shape[1], per_core, model_width)
        both = jnp.einsum("ned,egdf->gnef", flat, gate_up_here, preferred_element_type=jnp.float32)
        hidden = (jax.nn.silu(both[0]) * both[1]).astype(jnp.bfloat16)
        down = jnp.einsum("nef,efd->ned", hidden, down_here, preferred_element_type=jnp.float32)
        return down.astype(jnp.bfloat16).reshape(rows.shape)

    arrived = {0: rows_here}
    for step in range(1, req_total):
        if step == 3:
            arrived[step] = partner_move(arrived[1], 2)
        else:
            arrived[step] = partner_move(rows_here, step)
    plan = [[0], [1, 2]] + ([list(range(3, req_total))] if req_total > 3 else [])
    plan = [[k for k in group if k < req_total] for group in plan]
    returned = []
    previous = None
    for group in plan:
        if not group:
            continue
        inputs = [arrived[k] for k in group]
        if previous is not None:
            inputs, previous = lax.optimization_barrier((inputs, previous))
        outs = experts_on(jnp.stack(inputs, axis=0))
        previous = outs
        for slot_index, step in enumerate(group):
            part = outs[slot_index]
            returned.append(part if step == 0 else partner_move(part, step))
    token_weights = jnp.sum(own_combine, axis=-1)
    dispatch_bf = own_dispatch.astype(jnp.bfloat16)

    def pick(dispatch_part, parts):
        return sum(
            jnp.einsum("tec,ced->ted", dispatch_part, part, preferred_element_type=jnp.float32)
            for part in parts
        )

    if split:
        stacked = jnp.stack(returned, axis=0)
        kept = stacked[:, :capacity]
        came = lax.ppermute(stacked[:, capacity:], "dev", swap)
        moe_out = jnp.sum(
            lax.dynamic_slice_in_dim(token_weights, mine_first, per_core, 1)[:, :, None]
            * pick(lax.dynamic_slice_in_dim(dispatch_bf, mine_first, per_core, 1), list(kept)),
            axis=1,
        ) + jnp.sum(
            lax.dynamic_slice_in_dim(token_weights, other_first, per_core, 1)[:, :, None]
            * pick(lax.dynamic_slice_in_dim(dispatch_bf, other_first, per_core, 1), list(came)),
            axis=1,
        )
    else:
        selected = pick(dispatch_bf, returned)
        moe_out = jnp.sum(token_weights[:, :, None] * selected, axis=1)
    summed = lax.psum_scatter(
        moe_out.astype(jnp.bfloat16), "head", scatter_dimension=0, tiled=True
    ).astype(jnp.float32)
    rows_out = summed.shape[0]
    kept_rows = lax.dynamic_slice_in_dim(residual, head_index * rows_out, rows_out, 0)
    layer_out = (
        (kept_rows.astype(jnp.float32) + summed)
        .astype(jnp.bfloat16)
        .reshape(1, 1, rows_out, model_width)
    )
    owners_total = lax.axis_size("req")
    block_total = block_owner.shape[1]
    finished_total = block_owner.shape[0]
    per_owner = block_total // owners_total
    block_ids = jnp.arange(block_total, dtype=jnp.int32)
    same_owner = block_owner[:, :, None] == block_owner[:, None, :]
    before_mask = block_ids[None, :] < block_ids[:, None]
    page_rank = jnp.sum((same_owner & before_mask[None]).astype(jnp.int32), axis=2)
    own_owner = lax.dynamic_index_in_dim(block_owner, req_index, 0, keepdims=False)
    own_rank = lax.dynamic_index_in_dim(page_rank, req_index, 0, keepdims=False)
    dest_place = own_owner * per_owner + own_rank
    source_block = jnp.sum(
        jnp.where(dest_place[None, :] == block_ids[:, None], block_ids[None, :], 0), axis=1
    )
    page_half = kv_cache.shape[2]
    page_size = page_half * lax.axis_size("dev")
    token_pos = (
        block_ids[:, None] * page_size
        + dev_index * page_half
        + jnp.arange(page_half, dtype=jnp.int32)[None, :]
    )
    own_length = lax.dynamic_index_in_dim(lengths, req_index, 0, keepdims=False)
    live_cache = jnp.where(
        (token_pos < own_length)[:, :, None, None], kv_cache[0], jnp.zeros((), jnp.bfloat16)
    )
    outgoing = jnp.take(live_cache, source_block, axis=0)
    received = lax.all_to_all(outgoing, "req", split_axis=0, concat_axis=0, tiled=True)
    request_ids = jnp.arange(finished_total, dtype=jnp.int32)
    arrive_place = request_ids[:, None] * per_owner + page_rank
    own_blocks = block_owner == req_index
    slot_match = own_blocks[None] & (block_slot[None] == block_ids[:, None, None])
    gather_place = jnp.sum(jnp.where(slot_match, arrive_place[None], 0), axis=(1, 2))
    page_pool = jnp.take(received, gather_place, axis=0)
    return (layer_out, page_pool)


def solution(mesh):
    return jax.shard_map(
        body,
        mesh=mesh,
        in_specs=(
            P("req", "dev", None),
            P(),
            P(None, None, "head"),
            P("head", None),
            P(),
            P(None, "dev", None),
            P(None, "dev", None),
            P("head", None, None, "req"),
            P("head", "req", None),
            P("req", None, "dev", None, "head"),
            P(),
            P(),
            P(),
        ),
        out_specs=(P("req", "dev", "head", None), P("req", "dev", None, "head")),
        check_vma=False,
    )
```

```python
import jax
import jax.numpy as jnp
from jax import lax
from jax.sharding import PartitionSpec as P

EXPERTS = 8
HD = 64


def shifted(block, axis, distance):
    devices = range(lax.axis_size(axis))
    route = [(i - distance, i) for i in devices if i - distance in devices]
    return lax.ppermute(block, axis, route)


def norm_rows(values, gain_vec):
    widened = values.astype(jnp.float32)
    inv_rms = lax.rsqrt(jnp.mean(widened * widened, axis=-1, keepdims=True) + 1e-05)
    return (widened * inv_rms * gain_vec).astype(jnp.bfloat16)


def rotate(values, positions):
    half_dim = values.shape[-1] // 2
    frequency = 10000.0 ** (-jnp.arange(half_dim, dtype=jnp.float32) / half_dim)
    angles = positions[:, None] * frequency[None, :]
    cosine = jnp.cos(angles)[:, None, :]
    sine_part = jnp.sin(angles)[:, None, :]
    front_half = values[..., :half_dim]
    back_half = values[..., half_dim:]
    return jnp.concatenate(
        [front_half * cosine - back_half * sine_part, back_half * cosine + front_half * sine_part],
        axis=-1,
    )


def slot_tables(route_ids, weights, first_expert, experts_here, capacity):
    expert_ids = first_expert + jnp.arange(experts_here, dtype=jnp.int32)
    matches = (route_ids[..., None] == expert_ids).astype(jnp.float32)
    hit_shape = matches.shape
    flat_hits = matches.reshape(hit_shape[:-3] + (hit_shape[-3] * hit_shape[-2], hit_shape[-1]))
    ranking = (jnp.cumsum(flat_hits, axis=-2) - flat_hits).reshape(hit_shape)
    places = (ranking[..., None] == jnp.arange(capacity, dtype=jnp.float32)).astype(
        jnp.float32
    ) * matches[..., None]
    dispatch = jnp.sum(places, axis=-3)
    combine = jnp.sum(places * weights[..., None, None], axis=-3)
    return (dispatch, combine)


def hand_over_pages(kv_cache, lengths, block_owner, block_slot):
    dev_index = lax.axis_index("dev")
    req_index = lax.axis_index("req")
    owners_total = lax.axis_size("req")
    block_total = block_owner.shape[1]
    finished_total = block_owner.shape[0]
    per_owner = block_total // owners_total
    block_ids = jnp.arange(block_total, dtype=jnp.int32)
    same_owner = block_owner[:, :, None] == block_owner[:, None, :]
    before_mask = block_ids[None, :] < block_ids[:, None]
    page_rank = jnp.sum((same_owner & before_mask[None]).astype(jnp.int32), axis=2)
    own_owner = lax.dynamic_index_in_dim(block_owner, req_index, 0, keepdims=False)
    own_rank = lax.dynamic_index_in_dim(page_rank, req_index, 0, keepdims=False)
    dest_place = own_owner * per_owner + own_rank
    source_block = jnp.sum(
        jnp.where(dest_place[None, :] == block_ids[:, None], block_ids[None, :], 0), axis=1
    )
    page_half = kv_cache.shape[2]
    page_size = page_half * lax.axis_size("dev")
    token_pos = (
        block_ids[:, None] * page_size
        + dev_index * page_half
        + jnp.arange(page_half, dtype=jnp.int32)[None, :]
    )
    own_length = lax.dynamic_index_in_dim(lengths, req_index, 0, keepdims=False)
    live_cache = jnp.where(
        (token_pos < own_length)[:, :, None, None], kv_cache[0], jnp.zeros((), jnp.bfloat16)
    )
    outgoing = jnp.take(live_cache, source_block, axis=0)
    received = lax.all_to_all(outgoing, "req", split_axis=0, concat_axis=0, tiled=True)
    request_ids = jnp.arange(finished_total, dtype=jnp.int32)
    arrive_place = request_ids[:, None] * per_owner + page_rank
    own_blocks = block_owner == req_index
    slot_match = own_blocks[None] & (block_slot[None] == block_ids[:, None, None])
    gather_place = jnp.sum(jnp.where(slot_match, arrive_place[None], 0), axis=(1, 2))
    page_pool = jnp.take(received, gather_place, axis=0)
    return page_pool


def body(
    tokens,
    attn_gain,
    w_qkv,
    w_out,
    moe_gain,
    routes,
    route_weight,
    w_gate_up,
    w_down,
    kv_cache,
    lengths,
    block_owner,
    block_slot,
):
    half_rows = tokens.shape[1]
    model_width = tokens.shape[2]
    dev_index = lax.axis_index("dev")
    req_index = lax.axis_index("req")
    head_index = lax.axis_index("head")
    local_cols = w_qkv.shape[2]
    head_count = local_cols // HD
    normed = norm_rows(tokens[0], attn_gain)
    projected = jnp.dot(
        normed, w_qkv.reshape(model_width, 3 * local_cols), preferred_element_type=jnp.float32
    ).reshape(half_rows, 3, head_count, HD)
    query_pos = dev_index * half_rows + jnp.arange(half_rows, dtype=jnp.int32)
    angles_at = query_pos.astype(jnp.float32)
    queries = rotate(projected[:, 0], angles_at).astype(jnp.bfloat16)
    key_rows = rotate(projected[:, 1], angles_at).astype(jnp.bfloat16)
    values = projected[:, 2].astype(jnp.bfloat16)
    earlier_keys, earlier_values = shifted((key_rows, values), "dev", 1)
    all_keys = jnp.concatenate([earlier_keys, key_rows], axis=0)
    all_values = jnp.concatenate([earlier_values, values], axis=0)
    key_pos = (dev_index - 1) * half_rows + jnp.arange(2 * half_rows, dtype=jnp.int32)
    allowed = (key_pos[None, :] <= query_pos[:, None]) & (key_pos[None, :] >= 0)
    scores = (
        jnp.einsum("qhd,khd->hqk", queries, all_keys, preferred_element_type=jnp.float32) * 0.125
    )
    scores = jnp.where(allowed[None], scores, -1e30)
    row_peak = jnp.max(scores, axis=-1, keepdims=True)
    exp_scores = jnp.exp(scores - row_peak)
    row_total = jnp.sum(exp_scores, axis=-1)
    attended = (
        jnp.einsum(
            "hqk,khd->qhd",
            exp_scores.astype(jnp.bfloat16),
            all_values,
            preferred_element_type=jnp.float32,
        )
        / jnp.transpose(row_total)[:, :, None]
    )
    attended = attended.astype(jnp.bfloat16).reshape(half_rows, local_cols)
    partial_value = jnp.dot(attended, w_out, preferred_element_type=jnp.float32)
    reduced_in = partial_value.astype(jnp.bfloat16)
    attn_mixed = lax.psum(reduced_in, "head").astype(jnp.float32)
    kv_cache, reduced_in = lax.optimization_barrier((kv_cache, reduced_in))
    page_pool = hand_over_pages(kv_cache, lengths, block_owner, block_slot)
    residual = (tokens[0].astype(jnp.float32) + attn_mixed).astype(jnp.bfloat16)
    moe_in = norm_rows(residual, moe_gain)
    experts_here = w_gate_up.shape[0]
    first_expert = head_index * experts_here
    top_count = routes.shape[2]
    capacity = half_rows * top_count * 3 // (2 * EXPERTS)
    own_routes = lax.dynamic_index_in_dim(routes, req_index, 0, keepdims=True)
    own_weights = lax.dynamic_index_in_dim(route_weight, req_index, 0, keepdims=True)
    own_dispatch, own_combine = slot_tables(
        own_routes, own_weights, first_expert, experts_here, capacity
    )
    own_dispatch = own_dispatch[0]
    own_combine = own_combine[0]
    picked_own = jnp.einsum(
        "tec,td->ced",
        own_dispatch.astype(jnp.bfloat16),
        moe_in,
        preferred_element_type=jnp.float32,
    ).astype(jnp.bfloat16)
    picked_own, page_pool = lax.optimization_barrier((picked_own, page_pool))
    req_total = lax.axis_size("req")

    def partner_move(block, step):
        return lax.ppermute(block, "req", [(i, i ^ step) for i in range(req_total)])

    def experts_on(rows):
        groups = rows.shape[0]
        flat = rows.reshape(groups * capacity, experts_here, model_width)
        both = jnp.einsum("ned,egdf->gnef", flat, w_gate_up, preferred_element_type=jnp.float32)
        hidden = (jax.nn.silu(both[0]) * both[1]).astype(jnp.bfloat16)
        down = jnp.einsum("nef,efd->ned", hidden, w_down, preferred_element_type=jnp.float32)
        return down.astype(jnp.bfloat16).reshape(groups, capacity, experts_here, model_width)

    arrived = {0: picked_own}
    for step in range(1, req_total):
        if step == 3:
            arrived[step] = partner_move(arrived[1], 2)
        else:
            arrived[step] = partner_move(picked_own, step)
    plan = [[0], [1, 2]] + ([list(range(3, req_total))] if req_total > 3 else [])
    plan = [[k for k in group if k < req_total] for group in plan]
    returned = []
    for group in plan:
        if not group:
            continue
        outs = experts_on(jnp.stack([arrived[k] for k in group], axis=0))
        for slot_index, step in enumerate(group):
            part = outs[slot_index]
            returned.append(part if step == 0 else partner_move(part, step))
    token_weights = jnp.sum(own_combine, axis=-1)
    dispatch_bf = own_dispatch.astype(jnp.bfloat16)
    selected = sum(
        jnp.einsum("tec,ced->ted", dispatch_bf, part, preferred_element_type=jnp.float32)
        for part in returned
    )
    moe_out = jnp.sum(token_weights[:, :, None] * selected, axis=1)
    summed = lax.psum_scatter(
        moe_out.astype(jnp.bfloat16), "head", scatter_dimension=0, tiled=True
    ).astype(jnp.float32)
    rows_out = summed.shape[0]
    kept_rows = lax.dynamic_slice_in_dim(residual, head_index * rows_out, rows_out, 0)
    layer_out = (
        (kept_rows.astype(jnp.float32) + summed)
        .astype(jnp.bfloat16)
        .reshape(1, 1, rows_out, model_width)
    )
    return (layer_out, page_pool)


def solution(mesh):
    return jax.shard_map(
        body,
        mesh=mesh,
        in_specs=(
            P("req", "dev", None),
            P(),
            P(None, None, "head"),
            P("head", None),
            P(),
            P(None, "dev", None),
            P(None, "dev", None),
            P("head", None, None, "req"),
            P("head", "req", None),
            P("req", None, "dev", None, "head"),
            P(),
            P(),
            P(),
        ),
        out_specs=(P("req", "dev", "head", None), P("req", "dev", None, "head")),
        check_vma=False,
    )
```

```python
import jax
import jax.numpy as jnp
from jax import lax
from jax.sharding import PartitionSpec as P

EXPERTS = 8
HD = 64


def shifted(block, axis, distance):
    devices = range(lax.axis_size(axis))
    route = [(i - distance, i) for i in devices if i - distance in devices]
    return lax.ppermute(block, axis, route)


def norm_rows(values, gain_vec):
    widened = values.astype(jnp.float32)
    inv_rms = lax.rsqrt(jnp.mean(widened * widened, axis=-1, keepdims=True) + 1e-05)
    return (widened * inv_rms * gain_vec).astype(jnp.bfloat16)


def rotate(values, positions):
    half_dim = values.shape[-1] // 2
    frequency = 10000.0 ** (-jnp.arange(half_dim, dtype=jnp.float32) / half_dim)
    angles = positions[:, None] * frequency[None, :]
    cosine = jnp.cos(angles)[:, None, :]
    sine_part = jnp.sin(angles)[:, None, :]
    front_half = values[..., :half_dim]
    back_half = values[..., half_dim:]
    return jnp.concatenate(
        [front_half * cosine - back_half * sine_part, back_half * cosine + front_half * sine_part],
        axis=-1,
    )


def slot_tables(route_ids, weights, first_expert, experts_here, capacity):
    expert_ids = first_expert + jnp.arange(experts_here, dtype=jnp.int32)
    matches = (route_ids[..., None] == expert_ids).astype(jnp.float32)
    hit_shape = matches.shape
    flat_hits = matches.reshape(hit_shape[:-3] + (hit_shape[-3] * hit_shape[-2], hit_shape[-1]))
    ranking = (jnp.cumsum(flat_hits, axis=-2) - flat_hits).reshape(hit_shape)
    places = (ranking[..., None] == jnp.arange(capacity, dtype=jnp.float32)).astype(
        jnp.float32
    ) * matches[..., None]
    dispatch = jnp.sum(places, axis=-3)
    combine = jnp.sum(places * weights[..., None, None], axis=-3)
    return (dispatch, combine)


def body(
    tokens,
    attn_gain,
    w_qkv,
    w_out,
    moe_gain,
    routes,
    route_weight,
    w_gate_up,
    w_down,
    kv_cache,
    lengths,
    block_owner,
    block_slot,
):
    half_rows = tokens.shape[1]
    model_width = tokens.shape[2]
    dev_index = lax.axis_index("dev")
    req_index = lax.axis_index("req")
    head_index = lax.axis_index("head")
    local_cols = w_qkv.shape[2]
    head_count = local_cols // HD
    normed = norm_rows(tokens[0], attn_gain)
    projected = jnp.dot(
        normed, w_qkv.reshape(model_width, 3 * local_cols), preferred_element_type=jnp.float32
    ).reshape(half_rows, 3, head_count, HD)
    query_pos = dev_index * half_rows + jnp.arange(half_rows, dtype=jnp.int32)
    angles_at = query_pos.astype(jnp.float32)
    queries = rotate(projected[:, 0], angles_at).astype(jnp.bfloat16)
    key_rows = rotate(projected[:, 1], angles_at).astype(jnp.bfloat16)
    values = projected[:, 2].astype(jnp.bfloat16)
    earlier_keys, earlier_values = shifted((key_rows, values), "dev", 1)
    all_keys = jnp.concatenate([earlier_keys, key_rows], axis=0)
    all_values = jnp.concatenate([earlier_values, values], axis=0)
    key_pos = (dev_index - 1) * half_rows + jnp.arange(2 * half_rows, dtype=jnp.int32)
    allowed = (key_pos[None, :] <= query_pos[:, None]) & (key_pos[None, :] >= 0)
    scores = (
        jnp.einsum("qhd,khd->hqk", queries, all_keys, preferred_element_type=jnp.float32) * 0.125
    )
    scores = jnp.where(allowed[None], scores, -1e30)
    row_peak = jnp.max(scores, axis=-1, keepdims=True)
    exp_scores = jnp.exp(scores - row_peak)
    row_total = jnp.sum(exp_scores, axis=-1)
    attended = (
        jnp.einsum(
            "hqk,khd->qhd",
            exp_scores.astype(jnp.bfloat16),
            all_values,
            preferred_element_type=jnp.float32,
        )
        / jnp.transpose(row_total)[:, :, None]
    )
    attended = attended.astype(jnp.bfloat16).reshape(half_rows, local_cols)
    partial_value = jnp.dot(attended, w_out, preferred_element_type=jnp.float32)
    attn_mixed = lax.psum(partial_value.astype(jnp.bfloat16), "head").astype(jnp.float32)
    residual = (tokens[0].astype(jnp.float32) + attn_mixed).astype(jnp.bfloat16)
    moe_in = norm_rows(residual, moe_gain)
    experts_here = w_gate_up.shape[0]
    first_expert = head_index * experts_here
    top_count = routes.shape[2]
    capacity = half_rows * top_count * 3 // (2 * EXPERTS)
    own_routes = lax.dynamic_index_in_dim(routes, req_index, 0, keepdims=True)
    own_weights = lax.dynamic_index_in_dim(route_weight, req_index, 0, keepdims=True)
    own_dispatch, own_combine = slot_tables(
        own_routes, own_weights, first_expert, experts_here, capacity
    )
    own_dispatch = own_dispatch[0]
    own_combine = own_combine[0]
    picked_own = jnp.einsum(
        "tec,td->ced",
        own_dispatch.astype(jnp.bfloat16),
        moe_in,
        preferred_element_type=jnp.float32,
    ).astype(jnp.bfloat16)
    req_total = lax.axis_size("req")

    def partner_move(block, step):
        return lax.ppermute(block, "req", [(i, i ^ step) for i in range(req_total)])

    def experts_on(rows):
        groups = rows.shape[0]
        flat = rows.reshape(groups * capacity, experts_here, model_width)
        both = jnp.einsum("ned,egdf->gnef", flat, w_gate_up, preferred_element_type=jnp.float32)
        hidden = (jax.nn.silu(both[0]) * both[1]).astype(jnp.bfloat16)
        down = jnp.einsum("nef,efd->ned", hidden, w_down, preferred_element_type=jnp.float32)
        return down.astype(jnp.bfloat16).reshape(groups, capacity, experts_here, model_width)

    arrived = {0: picked_own}
    for step in range(1, req_total):
        if step == 3:
            arrived[step] = partner_move(arrived[1], 2)
        else:
            arrived[step] = partner_move(picked_own, step)
    plan = [[0], [1, 2]] + ([list(range(3, req_total))] if req_total > 3 else [])
    plan = [[k for k in group if k < req_total] for group in plan]
    returned = []
    for group in plan:
        if not group:
            continue
        outs = experts_on(jnp.stack([arrived[k] for k in group], axis=0))
        for slot_index, step in enumerate(group):
            part = outs[slot_index]
            returned.append(part if step == 0 else partner_move(part, step))
    token_weights = jnp.sum(own_combine, axis=-1)
    dispatch_bf = own_dispatch.astype(jnp.bfloat16)
    selected = sum(
        jnp.einsum("tec,ced->ted", dispatch_bf, part, preferred_element_type=jnp.float32)
        for part in returned
    )
    moe_out = jnp.sum(token_weights[:, :, None] * selected, axis=1)
    summed = lax.psum_scatter(
        moe_out.astype(jnp.bfloat16), "head", scatter_dimension=0, tiled=True
    ).astype(jnp.float32)
    rows_out = summed.shape[0]
    kept_rows = lax.dynamic_slice_in_dim(residual, head_index * rows_out, rows_out, 0)
    layer_out = (
        (kept_rows.astype(jnp.float32) + summed)
        .astype(jnp.bfloat16)
        .reshape(1, 1, rows_out, model_width)
    )
    owners_total = lax.axis_size("req")
    block_total = block_owner.shape[1]
    finished_total = block_owner.shape[0]
    per_owner = block_total // owners_total
    block_ids = jnp.arange(block_total, dtype=jnp.int32)
    same_owner = block_owner[:, :, None] == block_owner[:, None, :]
    before_mask = block_ids[None, :] < block_ids[:, None]
    page_rank = jnp.sum((same_owner & before_mask[None]).astype(jnp.int32), axis=2)
    own_owner = lax.dynamic_index_in_dim(block_owner, req_index, 0, keepdims=False)
    own_rank = lax.dynamic_index_in_dim(page_rank, req_index, 0, keepdims=False)
    dest_place = own_owner * per_owner + own_rank
    source_block = jnp.sum(
        jnp.where(dest_place[None, :] == block_ids[:, None], block_ids[None, :], 0), axis=1
    )
    page_half = kv_cache.shape[2]
    page_size = page_half * lax.axis_size("dev")
    token_pos = (
        block_ids[:, None] * page_size
        + dev_index * page_half
        + jnp.arange(page_half, dtype=jnp.int32)[None, :]
    )
    own_length = lax.dynamic_index_in_dim(lengths, req_index, 0, keepdims=False)
    live_cache = jnp.where(
        (token_pos < own_length)[:, :, None, None], kv_cache[0], jnp.zeros((), jnp.bfloat16)
    )
    outgoing = jnp.take(live_cache, source_block, axis=0, mode="clip")
    received = lax.all_to_all(outgoing, "req", split_axis=0, concat_axis=0, tiled=True)
    request_ids = jnp.arange(finished_total, dtype=jnp.int32)
    arrive_place = request_ids[:, None] * per_owner + page_rank
    own_blocks = block_owner == req_index
    slot_match = own_blocks[None] & (block_slot[None] == block_ids[:, None, None])
    gather_place = jnp.sum(jnp.where(slot_match, arrive_place[None], 0), axis=(1, 2))
    page_pool = jnp.take(received, gather_place, axis=0, mode="clip")
    return (layer_out, page_pool)


def solution(mesh):
    return jax.shard_map(
        body,
        mesh=mesh,
        in_specs=(
            P("req", "dev", None),
            P(),
            P(None, None, "head"),
            P("head", None),
            P(),
            P(None, "dev", None),
            P(None, "dev", None),
            P("head", None, None, "req"),
            P("head", "req", None),
            P("req", None, "dev", None, "head"),
            P(),
            P(),
            P(),
        ),
        out_specs=(P("req", "dev", "head", None), P("req", "dev", None, "head")),
        check_vma=False,
    )
```

```python
import jax
import jax.numpy as jnp
from jax import lax
from jax.sharding import PartitionSpec as P

EXPERTS = 8
HD = 64


def shifted(block, axis, distance):
    devices = range(lax.axis_size(axis))
    route = [(i - distance, i) for i in devices if i - distance in devices]
    return lax.ppermute(block, axis, route)


def norm_rows(values, gain_vec):
    widened = values.astype(jnp.float32)
    inv_rms = lax.rsqrt(jnp.mean(widened * widened, axis=-1, keepdims=True) + 1e-05)
    return (widened * inv_rms * gain_vec).astype(jnp.bfloat16)


def rotate(values, positions):
    half_dim = values.shape[-1] // 2
    frequency = 10000.0 ** (-jnp.arange(half_dim, dtype=jnp.float32) / half_dim)
    angles = positions[:, None] * frequency[None, :]
    cosine = jnp.cos(angles)[:, None, :]
    sine_part = jnp.sin(angles)[:, None, :]
    front_half = values[..., :half_dim]
    back_half = values[..., half_dim:]
    return jnp.concatenate(
        [front_half * cosine - back_half * sine_part, back_half * cosine + front_half * sine_part],
        axis=-1,
    )


def slot_tables(route_ids, weights, first_expert, experts_here, capacity):
    expert_ids = first_expert + jnp.arange(experts_here, dtype=jnp.int32)
    matches = (route_ids[..., None] == expert_ids).astype(jnp.float32)
    hit_shape = matches.shape
    flat_hits = matches.reshape(hit_shape[:-3] + (hit_shape[-3] * hit_shape[-2], hit_shape[-1]))
    ranking = (jnp.cumsum(flat_hits, axis=-2) - flat_hits).reshape(hit_shape)
    places = (ranking[..., None] == jnp.arange(capacity, dtype=jnp.float32)).astype(
        jnp.float32
    ) * matches[..., None]
    dispatch = jnp.sum(places, axis=-3)
    combine = jnp.sum(places * weights[..., None, None], axis=-3)
    return (dispatch, combine)


def pages_out(kv_cache, lengths, block_owner, block_slot):
    dev_index = lax.axis_index("dev")
    req_index = lax.axis_index("req")
    owners_total = lax.axis_size("req")
    block_total = block_owner.shape[1]
    finished_total = block_owner.shape[0]
    per_owner = block_total // owners_total
    block_ids = jnp.arange(block_total, dtype=jnp.int32)
    same_owner = block_owner[:, :, None] == block_owner[:, None, :]
    before_mask = block_ids[None, :] < block_ids[:, None]
    page_rank = jnp.sum((same_owner & before_mask[None]).astype(jnp.int32), axis=2)
    own_owner = lax.dynamic_index_in_dim(block_owner, req_index, 0, keepdims=False)
    own_rank = lax.dynamic_index_in_dim(page_rank, req_index, 0, keepdims=False)
    dest_place = own_owner * per_owner + own_rank
    source_block = jnp.sum(
        jnp.where(dest_place[None, :] == block_ids[:, None], block_ids[None, :], 0), axis=1
    )
    page_half = kv_cache.shape[2]
    page_size = page_half * lax.axis_size("dev")
    token_pos = (
        block_ids[:, None] * page_size
        + dev_index * page_half
        + jnp.arange(page_half, dtype=jnp.int32)[None, :]
    )
    own_length = lax.dynamic_index_in_dim(lengths, req_index, 0, keepdims=False)
    live_cache = jnp.where(
        (token_pos < own_length)[:, :, None, None], kv_cache[0], jnp.zeros((), jnp.bfloat16)
    )
    outgoing = jnp.take(live_cache, source_block, axis=0, mode="clip")
    return outgoing


def pages_in(outgoing, block_owner, block_slot):
    req_index = lax.axis_index("req")
    block_total = block_owner.shape[1]
    finished_total = block_owner.shape[0]
    per_owner = block_total // lax.axis_size("req")
    block_ids = jnp.arange(block_total, dtype=jnp.int32)
    same_owner = block_owner[:, :, None] == block_owner[:, None, :]
    before_mask = block_ids[None, :] < block_ids[:, None]
    page_rank = jnp.sum((same_owner & before_mask[None]).astype(jnp.int32), axis=2)
    received = lax.all_to_all(outgoing, "req", split_axis=0, concat_axis=0, tiled=True)
    request_ids = jnp.arange(finished_total, dtype=jnp.int32)
    arrive_place = request_ids[:, None] * per_owner + page_rank
    own_blocks = block_owner == req_index
    slot_match = own_blocks[None] & (block_slot[None] == block_ids[:, None, None])
    gather_place = jnp.sum(jnp.where(slot_match, arrive_place[None], 0), axis=(1, 2))
    page_pool = jnp.take(received, gather_place, axis=0, mode="clip")
    return page_pool


def body(
    tokens,
    attn_gain,
    w_qkv,
    w_out,
    moe_gain,
    routes,
    route_weight,
    w_gate_up,
    w_down,
    kv_cache,
    lengths,
    block_owner,
    block_slot,
):
    half_rows = tokens.shape[1]
    model_width = tokens.shape[2]
    dev_index = lax.axis_index("dev")
    req_index = lax.axis_index("req")
    head_index = lax.axis_index("head")
    local_cols = w_qkv.shape[2]
    head_count = local_cols // HD
    normed = norm_rows(tokens[0], attn_gain)
    projected = jnp.dot(
        normed, w_qkv.reshape(model_width, 3 * local_cols), preferred_element_type=jnp.float32
    ).reshape(half_rows, 3, head_count, HD)
    query_pos = dev_index * half_rows + jnp.arange(half_rows, dtype=jnp.int32)
    angles_at = query_pos.astype(jnp.float32)
    queries = rotate(projected[:, 0], angles_at).astype(jnp.bfloat16)
    key_rows = rotate(projected[:, 1], angles_at).astype(jnp.bfloat16)
    values = projected[:, 2].astype(jnp.bfloat16)
    earlier_keys, earlier_values = shifted((key_rows, values), "dev", 1)
    all_keys = jnp.concatenate([earlier_keys, key_rows], axis=0)
    all_values = jnp.concatenate([earlier_values, values], axis=0)
    key_pos = (dev_index - 1) * half_rows + jnp.arange(2 * half_rows, dtype=jnp.int32)
    allowed = (key_pos[None, :] <= query_pos[:, None]) & (key_pos[None, :] >= 0)
    scores = (
        jnp.einsum("qhd,khd->hqk", queries, all_keys, preferred_element_type=jnp.float32) * 0.125
    )
    scores = jnp.where(allowed[None], scores, -1e30)
    row_peak = jnp.max(scores, axis=-1, keepdims=True)
    exp_scores = jnp.exp(scores - row_peak)
    row_total = jnp.sum(exp_scores, axis=-1)
    attended = (
        jnp.einsum(
            "hqk,khd->qhd",
            exp_scores.astype(jnp.bfloat16),
            all_values,
            preferred_element_type=jnp.float32,
        )
        / jnp.transpose(row_total)[:, :, None]
    )
    attended = attended.astype(jnp.bfloat16).reshape(half_rows, local_cols)
    partial_value = jnp.dot(attended, w_out, preferred_element_type=jnp.float32)
    attn_mixed = lax.psum(partial_value.astype(jnp.bfloat16), "head").astype(jnp.float32)
    residual = (tokens[0].astype(jnp.float32) + attn_mixed).astype(jnp.bfloat16)
    moe_in = norm_rows(residual, moe_gain)
    outgoing = pages_out(kv_cache, lengths, block_owner, block_slot)
    moe_in, outgoing = lax.optimization_barrier((moe_in, outgoing))
    experts_here = w_gate_up.shape[0]
    first_expert = head_index * experts_here
    top_count = routes.shape[2]
    capacity = half_rows * top_count * 3 // (2 * EXPERTS)
    own_routes = lax.dynamic_index_in_dim(routes, req_index, 0, keepdims=True)
    own_weights = lax.dynamic_index_in_dim(route_weight, req_index, 0, keepdims=True)
    own_dispatch, own_combine = slot_tables(
        own_routes, own_weights, first_expert, experts_here, capacity
    )
    own_dispatch = own_dispatch[0]
    own_combine = own_combine[0]
    picked_own = jnp.einsum(
        "tec,td->ced",
        own_dispatch.astype(jnp.bfloat16),
        moe_in,
        preferred_element_type=jnp.float32,
    ).astype(jnp.bfloat16)
    req_total = lax.axis_size("req")

    def partner_move(block, step):
        return lax.ppermute(block, "req", [(i, i ^ step) for i in range(req_total)])

    def experts_on(rows):
        groups = rows.shape[0]
        flat = rows.reshape(groups * capacity, experts_here, model_width)
        both = jnp.einsum("ned,egdf->gnef", flat, w_gate_up, preferred_element_type=jnp.float32)
        hidden = (jax.nn.silu(both[0]) * both[1]).astype(jnp.bfloat16)
        down = jnp.einsum("nef,efd->ned", hidden, w_down, preferred_element_type=jnp.float32)
        return down.astype(jnp.bfloat16).reshape(groups, capacity, experts_here, model_width)

    arrived = {0: picked_own}
    for step in range(1, req_total):
        if step == 3:
            arrived[step] = partner_move(arrived[1], 2)
        else:
            arrived[step] = partner_move(picked_own, step)
    plan = [[0], [1, 2]] + ([list(range(3, req_total))] if req_total > 3 else [])
    plan = [[k for k in group if k < req_total] for group in plan]
    returned = []
    for group in plan:
        if not group:
            continue
        outs = experts_on(jnp.stack([arrived[k] for k in group], axis=0))
        for slot_index, step in enumerate(group):
            part = outs[slot_index]
            returned.append(part if step == 0 else partner_move(part, step))
    token_weights = jnp.sum(own_combine, axis=-1)
    dispatch_bf = own_dispatch.astype(jnp.bfloat16)
    selected = sum(
        jnp.einsum("tec,ced->ted", dispatch_bf, part, preferred_element_type=jnp.float32)
        for part in returned
    )
    moe_out = jnp.sum(token_weights[:, :, None] * selected, axis=1)
    summed = lax.psum_scatter(
        moe_out.astype(jnp.bfloat16), "head", scatter_dimension=0, tiled=True
    ).astype(jnp.float32)
    rows_out = summed.shape[0]
    kept_rows = lax.dynamic_slice_in_dim(residual, head_index * rows_out, rows_out, 0)
    layer_out = (
        (kept_rows.astype(jnp.float32) + summed)
        .astype(jnp.bfloat16)
        .reshape(1, 1, rows_out, model_width)
    )
    page_pool = pages_in(outgoing, block_owner, block_slot)
    return (layer_out, page_pool)


def solution(mesh):
    return jax.shard_map(
        body,
        mesh=mesh,
        in_specs=(
            P("req", "dev", None),
            P(),
            P(None, None, "head"),
            P("head", None),
            P(),
            P(None, "dev", None),
            P(None, "dev", None),
            P("head", None, None, "req"),
            P("head", "req", None),
            P("req", None, "dev", None, "head"),
            P(),
            P(),
            P(),
        ),
        out_specs=(P("req", "dev", "head", None), P("req", "dev", None, "head")),
        check_vma=False,
    )
```

```python
import jax
import jax.numpy as jnp
from jax import lax
from jax.sharding import PartitionSpec as P

EXPERTS = 8
HD = 64


def shifted(block, axis, distance):
    devices = range(lax.axis_size(axis))
    route = [(i - distance, i) for i in devices if i - distance in devices]
    return lax.ppermute(block, axis, route)


def norm_rows(values, gain_vec):
    widened = values.astype(jnp.float32)
    inv_rms = lax.rsqrt(jnp.mean(widened * widened, axis=-1, keepdims=True) + 1e-05)
    return (widened * inv_rms * gain_vec).astype(jnp.bfloat16)


def rotate(values, positions):
    half_dim = values.shape[-1] // 2
    frequency = 10000.0 ** (-jnp.arange(half_dim, dtype=jnp.float32) / half_dim)
    angles = positions[:, None] * frequency[None, :]
    cosine = jnp.cos(angles)[:, None, :]
    sine_part = jnp.sin(angles)[:, None, :]
    front_half = values[..., :half_dim]
    back_half = values[..., half_dim:]
    return jnp.concatenate(
        [front_half * cosine - back_half * sine_part, back_half * cosine + front_half * sine_part],
        axis=-1,
    )


def slot_tables(route_ids, weights, first_expert, experts_here, capacity):
    expert_ids = first_expert + jnp.arange(experts_here, dtype=jnp.int32)
    matches = (route_ids[..., None] == expert_ids).astype(jnp.float32)
    hit_shape = matches.shape
    flat_hits = matches.reshape(hit_shape[:-3] + (hit_shape[-3] * hit_shape[-2], hit_shape[-1]))
    ranking = (jnp.cumsum(flat_hits, axis=-2) - flat_hits).reshape(hit_shape)
    places = (ranking[..., None] == jnp.arange(capacity, dtype=jnp.float32)).astype(
        jnp.float32
    ) * matches[..., None]
    dispatch = jnp.sum(places, axis=-3)
    combine = jnp.sum(places * weights[..., None, None], axis=-3)
    return (dispatch, combine)


def pages_out(kv_cache, lengths, block_owner, block_slot):
    dev_index = lax.axis_index("dev")
    req_index = lax.axis_index("req")
    owners_total = lax.axis_size("req")
    block_total = block_owner.shape[1]
    finished_total = block_owner.shape[0]
    per_owner = block_total // owners_total
    block_ids = jnp.arange(block_total, dtype=jnp.int32)
    same_owner = block_owner[:, :, None] == block_owner[:, None, :]
    before_mask = block_ids[None, :] < block_ids[:, None]
    page_rank = jnp.sum((same_owner & before_mask[None]).astype(jnp.int32), axis=2)
    own_owner = lax.dynamic_index_in_dim(block_owner, req_index, 0, keepdims=False)
    own_rank = lax.dynamic_index_in_dim(page_rank, req_index, 0, keepdims=False)
    dest_place = own_owner * per_owner + own_rank
    source_block = jnp.sum(
        jnp.where(dest_place[None, :] == block_ids[:, None], block_ids[None, :], 0), axis=1
    )
    page_half = kv_cache.shape[2]
    page_size = page_half * lax.axis_size("dev")
    token_pos = (
        block_ids[:, None] * page_size
        + dev_index * page_half
        + jnp.arange(page_half, dtype=jnp.int32)[None, :]
    )
    own_length = lax.dynamic_index_in_dim(lengths, req_index, 0, keepdims=False)
    live_cache = jnp.where(
        (token_pos < own_length)[:, :, None, None], kv_cache[0], jnp.zeros((), jnp.bfloat16)
    )
    outgoing = jnp.take(live_cache, source_block, axis=0, mode="clip")
    return outgoing


def pages_in(outgoing, block_owner, block_slot):
    req_index = lax.axis_index("req")
    block_total = block_owner.shape[1]
    finished_total = block_owner.shape[0]
    per_owner = block_total // lax.axis_size("req")
    block_ids = jnp.arange(block_total, dtype=jnp.int32)
    same_owner = block_owner[:, :, None] == block_owner[:, None, :]
    before_mask = block_ids[None, :] < block_ids[:, None]
    page_rank = jnp.sum((same_owner & before_mask[None]).astype(jnp.int32), axis=2)
    received = lax.all_to_all(outgoing, "req", split_axis=0, concat_axis=0, tiled=True)
    request_ids = jnp.arange(finished_total, dtype=jnp.int32)
    arrive_place = request_ids[:, None] * per_owner + page_rank
    own_blocks = block_owner == req_index
    slot_match = own_blocks[None] & (block_slot[None] == block_ids[:, None, None])
    gather_place = jnp.sum(jnp.where(slot_match, arrive_place[None], 0), axis=(1, 2))
    page_pool = jnp.take(received, gather_place, axis=0, mode="clip")
    return page_pool


def body(
    tokens,
    attn_gain,
    w_qkv,
    w_out,
    moe_gain,
    routes,
    route_weight,
    w_gate_up,
    w_down,
    kv_cache,
    lengths,
    block_owner,
    block_slot,
):
    half_rows = tokens.shape[1]
    model_width = tokens.shape[2]
    dev_index = lax.axis_index("dev")
    req_index = lax.axis_index("req")
    head_index = lax.axis_index("head")
    local_cols = w_qkv.shape[2]
    head_count = local_cols // HD
    normed = norm_rows(tokens[0], attn_gain)
    projected = jnp.dot(
        normed, w_qkv.reshape(model_width, 3 * local_cols), preferred_element_type=jnp.float32
    ).reshape(half_rows, 3, head_count, HD)
    query_pos = dev_index * half_rows + jnp.arange(half_rows, dtype=jnp.int32)
    angles_at = query_pos.astype(jnp.float32)
    queries = rotate(projected[:, 0], angles_at).astype(jnp.bfloat16)
    key_rows = rotate(projected[:, 1], angles_at).astype(jnp.bfloat16)
    values = projected[:, 2].astype(jnp.bfloat16)
    earlier_both = shifted(jnp.stack([key_rows, values], axis=0), "dev", 1)
    earlier_keys, earlier_values = earlier_both[0], earlier_both[1]
    all_keys = jnp.concatenate([earlier_keys, key_rows], axis=0)
    all_values = jnp.concatenate([earlier_values, values], axis=0)
    key_pos = (dev_index - 1) * half_rows + jnp.arange(2 * half_rows, dtype=jnp.int32)
    allowed = (key_pos[None, :] <= query_pos[:, None]) & (key_pos[None, :] >= 0)
    scores = (
        jnp.einsum("qhd,khd->hqk", queries, all_keys, preferred_element_type=jnp.float32) * 0.125
    )
    scores = jnp.where(allowed[None], scores, -1e30)
    row_peak = jnp.max(scores, axis=-1, keepdims=True)
    exp_scores = jnp.exp(scores - row_peak)
    row_total = jnp.sum(exp_scores, axis=-1)
    attended = (
        jnp.einsum(
            "hqk,khd->qhd",
            exp_scores.astype(jnp.bfloat16),
            all_values,
            preferred_element_type=jnp.float32,
        )
        / jnp.transpose(row_total)[:, :, None]
    )
    attended = attended.astype(jnp.bfloat16).reshape(half_rows, local_cols)
    partial_value = jnp.dot(attended, w_out, preferred_element_type=jnp.float32)
    attn_mixed = lax.psum(partial_value.astype(jnp.bfloat16), "head").astype(jnp.float32)
    residual = (tokens[0].astype(jnp.float32) + attn_mixed).astype(jnp.bfloat16)
    moe_in = norm_rows(residual, moe_gain)
    outgoing = pages_out(kv_cache, lengths, block_owner, block_slot)
    moe_in, outgoing = lax.optimization_barrier((moe_in, outgoing))
    experts_here = w_gate_up.shape[0]
    first_expert = head_index * experts_here
    top_count = routes.shape[2]
    capacity = half_rows * top_count * 3 // (2 * EXPERTS)
    own_routes = lax.dynamic_index_in_dim(routes, req_index, 0, keepdims=True)
    own_weights = lax.dynamic_index_in_dim(route_weight, req_index, 0, keepdims=True)
    own_dispatch, own_combine = slot_tables(
        own_routes, own_weights, first_expert, experts_here, capacity
    )
    own_dispatch = own_dispatch[0]
    own_combine = own_combine[0]
    picked_own = jnp.einsum(
        "tec,td->ced",
        own_dispatch.astype(jnp.bfloat16),
        moe_in,
        preferred_element_type=jnp.float32,
    ).astype(jnp.bfloat16)
    req_total = lax.axis_size("req")

    def partner_move(block, step):
        return lax.ppermute(block, "req", [(i, i ^ step) for i in range(req_total)])

    def experts_on(rows):
        groups = rows.shape[0]
        flat = rows.reshape(groups * capacity, experts_here, model_width)
        both = jnp.einsum("ned,egdf->gnef", flat, w_gate_up, preferred_element_type=jnp.float32)
        hidden = (jax.nn.silu(both[0]) * both[1]).astype(jnp.bfloat16)
        down = jnp.einsum("nef,efd->ned", hidden, w_down, preferred_element_type=jnp.float32)
        return down.astype(jnp.bfloat16).reshape(groups, capacity, experts_here, model_width)

    arrived = {0: picked_own}
    for step in range(1, req_total):
        if step == 3:
            arrived[step] = partner_move(arrived[1], 2)
        else:
            arrived[step] = partner_move(picked_own, step)
    plan = [[0], [1, 2]] + ([list(range(3, req_total))] if req_total > 3 else [])
    plan = [[k for k in group if k < req_total] for group in plan]
    returned = []
    for group in plan:
        if not group:
            continue
        outs = experts_on(jnp.stack([arrived[k] for k in group], axis=0))
        for slot_index, step in enumerate(group):
            part = outs[slot_index]
            returned.append(part if step == 0 else partner_move(part, step))
    token_weights = jnp.sum(own_combine, axis=-1)
    dispatch_bf = own_dispatch.astype(jnp.bfloat16)
    selected = sum(
        jnp.einsum("tec,ced->ted", dispatch_bf, part, preferred_element_type=jnp.float32)
        for part in returned
    )
    moe_out = jnp.sum(token_weights[:, :, None] * selected, axis=1)
    summed = lax.psum_scatter(
        moe_out.astype(jnp.bfloat16), "head", scatter_dimension=0, tiled=True
    ).astype(jnp.float32)
    rows_out = summed.shape[0]
    kept_rows = lax.dynamic_slice_in_dim(residual, head_index * rows_out, rows_out, 0)
    layer_out = (
        (kept_rows.astype(jnp.float32) + summed)
        .astype(jnp.bfloat16)
        .reshape(1, 1, rows_out, model_width)
    )
    page_pool = pages_in(outgoing, block_owner, block_slot)
    return (layer_out, page_pool)


def solution(mesh):
    return jax.shard_map(
        body,
        mesh=mesh,
        in_specs=(
            P("req", "dev", None),
            P(),
            P(None, None, "head"),
            P("head", None),
            P(),
            P(None, "dev", None),
            P(None, "dev", None),
            P("head", None, None, "req"),
            P("head", "req", None),
            P("req", None, "dev", None, "head"),
            P(),
            P(),
            P(),
        ),
        out_specs=(P("req", "dev", "head", None), P("req", "dev", None, "head")),
        check_vma=False,
    )
```

```python
import jax
import jax.numpy as jnp
from jax import lax
from jax.sharding import PartitionSpec as P

EXPERTS = 8
HD = 64


def shifted(block, axis, distance):
    devices = range(lax.axis_size(axis))
    route = [(i - distance, i) for i in devices if i - distance in devices]
    return lax.ppermute(block, axis, route)


def norm_rows(values, gain_vec):
    widened = values.astype(jnp.float32)
    inv_rms = lax.rsqrt(jnp.mean(widened * widened, axis=-1, keepdims=True) + 1e-05)
    return (widened * inv_rms * gain_vec).astype(jnp.bfloat16)


def rotate(values, positions):
    half_dim = values.shape[-1] // 2
    frequency = 10000.0 ** (-jnp.arange(half_dim, dtype=jnp.float32) / half_dim)
    angles = positions[:, None] * frequency[None, :]
    cosine = jnp.cos(angles)[:, None, :]
    sine_part = jnp.sin(angles)[:, None, :]
    front_half = values[..., :half_dim]
    back_half = values[..., half_dim:]
    return jnp.concatenate(
        [front_half * cosine - back_half * sine_part, back_half * cosine + front_half * sine_part],
        axis=-1,
    )


def slot_tables(route_ids, weights, first_expert, experts_here, capacity):
    expert_ids = first_expert + jnp.arange(experts_here, dtype=jnp.int32)
    matches = (route_ids[..., None] == expert_ids).astype(jnp.float32)
    hit_shape = matches.shape
    flat_hits = matches.reshape(hit_shape[:-3] + (hit_shape[-3] * hit_shape[-2], hit_shape[-1]))
    ranking = (jnp.cumsum(flat_hits, axis=-2) - flat_hits).reshape(hit_shape)
    places = (ranking[..., None] == jnp.arange(capacity, dtype=jnp.float32)).astype(
        jnp.float32
    ) * matches[..., None]
    dispatch = jnp.sum(places, axis=-3)
    combine = jnp.sum(places * weights[..., None, None], axis=-3)
    return (dispatch, combine)


def pages_out(kv_cache, lengths, block_owner, block_slot):
    dev_index = lax.axis_index("dev")
    req_index = lax.axis_index("req")
    owners_total = lax.axis_size("req")
    block_total = block_owner.shape[1]
    finished_total = block_owner.shape[0]
    per_owner = block_total // owners_total
    block_ids = jnp.arange(block_total, dtype=jnp.int32)
    same_owner = block_owner[:, :, None] == block_owner[:, None, :]
    before_mask = block_ids[None, :] < block_ids[:, None]
    page_rank = jnp.sum((same_owner & before_mask[None]).astype(jnp.int32), axis=2)
    own_owner = lax.dynamic_index_in_dim(block_owner, req_index, 0, keepdims=False)
    own_rank = lax.dynamic_index_in_dim(page_rank, req_index, 0, keepdims=False)
    dest_place = own_owner * per_owner + own_rank
    source_block = jnp.sum(
        jnp.where(dest_place[None, :] == block_ids[:, None], block_ids[None, :], 0), axis=1
    )
    page_half = kv_cache.shape[2]
    page_size = page_half * lax.axis_size("dev")
    token_pos = (
        block_ids[:, None] * page_size
        + dev_index * page_half
        + jnp.arange(page_half, dtype=jnp.int32)[None, :]
    )
    own_length = lax.dynamic_index_in_dim(lengths, req_index, 0, keepdims=False)
    live_cache = jnp.where(
        (token_pos < own_length)[:, :, None, None], kv_cache[0], jnp.zeros((), jnp.bfloat16)
    )
    outgoing = jnp.take(live_cache, source_block, axis=0, mode="clip")
    return outgoing


def pages_in(outgoing, block_owner, block_slot):
    req_index = lax.axis_index("req")
    block_total = block_owner.shape[1]
    finished_total = block_owner.shape[0]
    per_owner = block_total // lax.axis_size("req")
    block_ids = jnp.arange(block_total, dtype=jnp.int32)
    same_owner = block_owner[:, :, None] == block_owner[:, None, :]
    before_mask = block_ids[None, :] < block_ids[:, None]
    page_rank = jnp.sum((same_owner & before_mask[None]).astype(jnp.int32), axis=2)
    received = lax.all_to_all(outgoing, "req", split_axis=0, concat_axis=0, tiled=True)
    request_ids = jnp.arange(finished_total, dtype=jnp.int32)
    arrive_place = request_ids[:, None] * per_owner + page_rank
    own_blocks = block_owner == req_index
    slot_match = own_blocks[None] & (block_slot[None] == block_ids[:, None, None])
    gather_place = jnp.sum(jnp.where(slot_match, arrive_place[None], 0), axis=(1, 2))
    page_pool = jnp.take(received, gather_place, axis=0, mode="clip")
    return page_pool


def body(
    tokens,
    attn_gain,
    w_qkv,
    w_out,
    moe_gain,
    routes,
    route_weight,
    w_gate_up,
    w_down,
    kv_cache,
    lengths,
    block_owner,
    block_slot,
):
    half_rows = tokens.shape[1]
    model_width = tokens.shape[2]
    dev_index = lax.axis_index("dev")
    req_index = lax.axis_index("req")
    head_index = lax.axis_index("head")
    local_cols = w_qkv.shape[2]
    head_count = local_cols // HD
    normed = norm_rows(tokens[0], attn_gain)
    projected = jnp.dot(
        normed, w_qkv.reshape(model_width, 3 * local_cols), preferred_element_type=jnp.float32
    ).reshape(half_rows, 3, head_count, HD)
    query_pos = dev_index * half_rows + jnp.arange(half_rows, dtype=jnp.int32)
    angles_at = query_pos.astype(jnp.float32)
    queries = rotate(projected[:, 0], angles_at).astype(jnp.bfloat16)
    key_rows = rotate(projected[:, 1], angles_at).astype(jnp.bfloat16)
    values = projected[:, 2].astype(jnp.bfloat16)
    earlier_both = shifted(jnp.stack([key_rows, values], axis=0), "dev", 1)
    earlier_keys, earlier_values = earlier_both[0], earlier_both[1]
    key_pos = (dev_index - 1) * half_rows + jnp.arange(2 * half_rows, dtype=jnp.int32)
    allowed = (key_pos[None, :] <= query_pos[:, None]) & (key_pos[None, :] >= 0)
    own_scores = jnp.einsum("qhd,khd->hqk", queries, key_rows, preferred_element_type=jnp.float32)
    early_scores = jnp.einsum(
        "qhd,khd->hqk", queries, earlier_keys, preferred_element_type=jnp.float32
    )
    scores = jnp.concatenate([early_scores, own_scores], axis=-1) * 0.125
    scores = jnp.where(allowed[None], scores, -1e30)
    row_peak = jnp.max(scores, axis=-1, keepdims=True)
    exp_scores = jnp.exp(scores - row_peak)
    row_total = jnp.sum(exp_scores, axis=-1)
    probs = exp_scores.astype(jnp.bfloat16)
    attended = (
        (
            jnp.einsum(
                "hqk,khd->qhd",
                probs[:, :, :half_rows],
                earlier_values,
                preferred_element_type=jnp.float32,
            )
            + jnp.einsum(
                "hqk,khd->qhd",
                probs[:, :, half_rows:],
                values,
                preferred_element_type=jnp.float32,
            )
        )
        / jnp.transpose(row_total)[:, :, None]
    )
    attended = attended.astype(jnp.bfloat16).reshape(half_rows, local_cols)
    partial_value = jnp.dot(attended, w_out, preferred_element_type=jnp.float32)
    attn_mixed = lax.psum(partial_value.astype(jnp.bfloat16), "head").astype(jnp.float32)
    residual = (tokens[0].astype(jnp.float32) + attn_mixed).astype(jnp.bfloat16)
    moe_in = norm_rows(residual, moe_gain)
    outgoing = pages_out(kv_cache, lengths, block_owner, block_slot)
    moe_in, outgoing = lax.optimization_barrier((moe_in, outgoing))
    experts_here = w_gate_up.shape[0]
    first_expert = head_index * experts_here
    top_count = routes.shape[2]
    capacity = half_rows * top_count * 3 // (2 * EXPERTS)
    own_routes = lax.dynamic_index_in_dim(routes, req_index, 0, keepdims=True)
    own_weights = lax.dynamic_index_in_dim(route_weight, req_index, 0, keepdims=True)
    own_dispatch, own_combine = slot_tables(
        own_routes, own_weights, first_expert, experts_here, capacity
    )
    own_dispatch = own_dispatch[0]
    own_combine = own_combine[0]
    picked_own = jnp.einsum(
        "tec,td->ced",
        own_dispatch.astype(jnp.bfloat16),
        moe_in,
        preferred_element_type=jnp.float32,
    ).astype(jnp.bfloat16)
    req_total = lax.axis_size("req")

    def partner_move(block, step):
        return lax.ppermute(block, "req", [(i, i ^ step) for i in range(req_total)])

    def experts_on(rows):
        groups = rows.shape[0]
        flat = rows.reshape(groups * capacity, experts_here, model_width)
        both = jnp.einsum("ned,egdf->gnef", flat, w_gate_up, preferred_element_type=jnp.float32)
        hidden = (jax.nn.silu(both[0]) * both[1]).astype(jnp.bfloat16)
        down = jnp.einsum("nef,efd->ned", hidden, w_down, preferred_element_type=jnp.float32)
        return down.astype(jnp.bfloat16).reshape(groups, capacity, experts_here, model_width)

    arrived = {0: picked_own}
    for step in range(1, req_total):
        if step == 3:
            arrived[step] = partner_move(arrived[1], 2)
        else:
            arrived[step] = partner_move(picked_own, step)
    plan = [[0], [1, 2]] + ([list(range(3, req_total))] if req_total > 3 else [])
    plan = [[k for k in group if k < req_total] for group in plan]
    returned = []
    for group in plan:
        if not group:
            continue
        outs = experts_on(jnp.stack([arrived[k] for k in group], axis=0))
        for slot_index, step in enumerate(group):
            part = outs[slot_index]
            returned.append(part if step == 0 else partner_move(part, step))
    token_weights = jnp.sum(own_combine, axis=-1)
    dispatch_bf = own_dispatch.astype(jnp.bfloat16)
    selected = sum(
        jnp.einsum("tec,ced->ted", dispatch_bf, part, preferred_element_type=jnp.float32)
        for part in returned
    )
    moe_out = jnp.sum(token_weights[:, :, None] * selected, axis=1)
    summed = lax.psum_scatter(
        moe_out.astype(jnp.bfloat16), "head", scatter_dimension=0, tiled=True
    ).astype(jnp.float32)
    rows_out = summed.shape[0]
    kept_rows = lax.dynamic_slice_in_dim(residual, head_index * rows_out, rows_out, 0)
    layer_out = (
        (kept_rows.astype(jnp.float32) + summed)
        .astype(jnp.bfloat16)
        .reshape(1, 1, rows_out, model_width)
    )
    page_pool = pages_in(outgoing, block_owner, block_slot)
    return (layer_out, page_pool)


def solution(mesh):
    return jax.shard_map(
        body,
        mesh=mesh,
        in_specs=(
            P("req", "dev", None),
            P(),
            P(None, None, "head"),
            P("head", None),
            P(),
            P(None, "dev", None),
            P(None, "dev", None),
            P("head", None, None, "req"),
            P("head", "req", None),
            P("req", None, "dev", None, "head"),
            P(),
            P(),
            P(),
        ),
        out_specs=(P("req", "dev", "head", None), P("req", "dev", None, "head")),
        check_vma=False,
    )
```

```python
import jax
import jax.numpy as jnp
from jax import lax
from jax.sharding import PartitionSpec as P

EXPERTS = 8
HD = 64


def shifted(block, axis, distance):
    devices = range(lax.axis_size(axis))
    route = [(i - distance, i) for i in devices if i - distance in devices]
    return lax.ppermute(block, axis, route)


def norm_rows(values, gain_vec):
    widened = values.astype(jnp.float32)
    inv_rms = lax.rsqrt(jnp.mean(widened * widened, axis=-1, keepdims=True) + 1e-05)
    return (widened * inv_rms * gain_vec).astype(jnp.bfloat16)


def rotate(values, positions):
    half_dim = values.shape[-1] // 2
    frequency = 10000.0 ** (-jnp.arange(half_dim, dtype=jnp.float32) / half_dim)
    angles = positions[:, None] * frequency[None, :]
    cosine = jnp.cos(angles)[:, None, :]
    sine_part = jnp.sin(angles)[:, None, :]
    front_half = values[..., :half_dim]
    back_half = values[..., half_dim:]
    return jnp.concatenate(
        [front_half * cosine - back_half * sine_part, back_half * cosine + front_half * sine_part],
        axis=-1,
    )


def slot_tables(route_ids, weights, first_expert, experts_here, capacity):
    expert_ids = first_expert + jnp.arange(experts_here, dtype=jnp.int32)
    matches = (route_ids[..., None] == expert_ids).astype(jnp.float32)
    hit_shape = matches.shape
    flat_hits = matches.reshape(hit_shape[:-3] + (hit_shape[-3] * hit_shape[-2], hit_shape[-1]))
    ranking = (jnp.cumsum(flat_hits, axis=-2) - flat_hits).reshape(hit_shape)
    places = (ranking[..., None] == jnp.arange(capacity, dtype=jnp.float32)).astype(
        jnp.float32
    ) * matches[..., None]
    dispatch = jnp.sum(places, axis=-3)
    combine = jnp.sum(places * weights[..., None, None], axis=-3)
    return (dispatch, combine)


def pages_out(kv_cache, lengths, block_owner, block_slot):
    dev_index = lax.axis_index("dev")
    req_index = lax.axis_index("req")
    owners_total = lax.axis_size("req")
    block_total = block_owner.shape[1]
    finished_total = block_owner.shape[0]
    per_owner = block_total // owners_total
    block_ids = jnp.arange(block_total, dtype=jnp.int32)
    same_owner = block_owner[:, :, None] == block_owner[:, None, :]
    before_mask = block_ids[None, :] < block_ids[:, None]
    page_rank = jnp.sum((same_owner & before_mask[None]).astype(jnp.int32), axis=2)
    own_owner = lax.dynamic_index_in_dim(block_owner, req_index, 0, keepdims=False)
    own_rank = lax.dynamic_index_in_dim(page_rank, req_index, 0, keepdims=False)
    dest_place = own_owner * per_owner + own_rank
    source_block = jnp.sum(
        jnp.where(dest_place[None, :] == block_ids[:, None], block_ids[None, :], 0), axis=1
    )
    page_half = kv_cache.shape[2]
    page_size = page_half * lax.axis_size("dev")
    token_pos = (
        block_ids[:, None] * page_size
        + dev_index * page_half
        + jnp.arange(page_half, dtype=jnp.int32)[None, :]
    )
    own_length = lax.dynamic_index_in_dim(lengths, req_index, 0, keepdims=False)
    live_cache = jnp.where(
        (token_pos < own_length)[:, :, None, None], kv_cache[0], jnp.zeros((), jnp.bfloat16)
    )
    outgoing = jnp.take(live_cache, source_block, axis=0, mode="clip")
    return outgoing


def pages_in(outgoing, block_owner, block_slot):
    req_index = lax.axis_index("req")
    block_total = block_owner.shape[1]
    finished_total = block_owner.shape[0]
    per_owner = block_total // lax.axis_size("req")
    block_ids = jnp.arange(block_total, dtype=jnp.int32)
    same_owner = block_owner[:, :, None] == block_owner[:, None, :]
    before_mask = block_ids[None, :] < block_ids[:, None]
    page_rank = jnp.sum((same_owner & before_mask[None]).astype(jnp.int32), axis=2)
    received = lax.all_to_all(outgoing, "req", split_axis=0, concat_axis=0, tiled=True)
    request_ids = jnp.arange(finished_total, dtype=jnp.int32)
    arrive_place = request_ids[:, None] * per_owner + page_rank
    own_blocks = block_owner == req_index
    slot_match = own_blocks[None] & (block_slot[None] == block_ids[:, None, None])
    gather_place = jnp.sum(jnp.where(slot_match, arrive_place[None], 0), axis=(1, 2))
    page_pool = jnp.take(received, gather_place, axis=0, mode="clip")
    return page_pool


def body(
    tokens,
    attn_gain,
    w_qkv,
    w_out,
    moe_gain,
    routes,
    route_weight,
    w_gate_up,
    w_down,
    kv_cache,
    lengths,
    block_owner,
    block_slot,
):
    half_rows = tokens.shape[1]
    model_width = tokens.shape[2]
    dev_index = lax.axis_index("dev")
    req_index = lax.axis_index("req")
    head_index = lax.axis_index("head")
    local_cols = w_qkv.shape[2]
    head_count = local_cols // HD
    normed = norm_rows(tokens[0], attn_gain)
    projected = jnp.dot(
        normed, w_qkv.reshape(model_width, 3 * local_cols), preferred_element_type=jnp.float32
    ).reshape(half_rows, 3, head_count, HD)
    query_pos = dev_index * half_rows + jnp.arange(half_rows, dtype=jnp.int32)
    angles_at = query_pos.astype(jnp.float32)
    queries = rotate(projected[:, 0], angles_at).astype(jnp.bfloat16)
    key_rows = rotate(projected[:, 1], angles_at).astype(jnp.bfloat16)
    values = projected[:, 2].astype(jnp.bfloat16)
    earlier_both = shifted(jnp.stack([key_rows, values], axis=0), "dev", 1)
    earlier_keys, earlier_values = earlier_both[0], earlier_both[1]
    all_keys = jnp.concatenate([earlier_keys, key_rows], axis=0)
    all_values = jnp.concatenate([earlier_values, values], axis=0)
    key_pos = (dev_index - 1) * half_rows + jnp.arange(2 * half_rows, dtype=jnp.int32)
    allowed = (key_pos[None, :] <= query_pos[:, None]) & (key_pos[None, :] >= 0)
    scores = (
        jnp.einsum("qhd,khd->hqk", queries, all_keys, preferred_element_type=jnp.float32) * 0.125
    )
    scores = jnp.where(allowed[None], scores, -1e30)
    row_peak = jnp.max(scores, axis=-1, keepdims=True)
    exp_scores = jnp.exp(scores - row_peak)
    row_total = jnp.sum(exp_scores, axis=-1)
    attended = (
        jnp.einsum(
            "hqk,khd->qhd",
            exp_scores.astype(jnp.bfloat16),
            all_values,
            preferred_element_type=jnp.float32,
        )
        / jnp.transpose(row_total)[:, :, None]
    )
    attended = attended.astype(jnp.bfloat16).reshape(half_rows, local_cols)
    partial_value = jnp.dot(attended, w_out, preferred_element_type=jnp.float32)
    attn_mixed = lax.psum(partial_value.astype(jnp.bfloat16), "head").astype(jnp.float32)
    residual = (tokens[0].astype(jnp.float32) + attn_mixed).astype(jnp.bfloat16)
    moe_in = norm_rows(residual, moe_gain)
    outgoing = pages_out(kv_cache, lengths, block_owner, block_slot)
    moe_in, outgoing = lax.optimization_barrier((moe_in, outgoing))
    experts_here = w_gate_up.shape[0]
    first_expert = head_index * experts_here
    top_count = routes.shape[2]
    capacity = half_rows * top_count * 3 // (2 * EXPERTS)
    own_routes = lax.dynamic_index_in_dim(routes, req_index, 0, keepdims=True)
    own_weights = lax.dynamic_index_in_dim(route_weight, req_index, 0, keepdims=True)
    own_dispatch, own_combine = slot_tables(
        own_routes, own_weights, first_expert, experts_here, capacity
    )
    own_dispatch = own_dispatch[0]
    own_combine = own_combine[0]
    picked_own = jnp.einsum(
        "tec,td->ced",
        own_dispatch.astype(jnp.bfloat16),
        moe_in,
        preferred_element_type=jnp.float32,
    ).astype(jnp.bfloat16)
    req_total = lax.axis_size("req")

    def partner_move(block, step):
        return lax.ppermute(block, "req", [(i, i ^ step) for i in range(req_total)])

    def experts_on(rows):
        groups = rows.shape[0]
        flat = rows.reshape(groups * capacity, experts_here, model_width)
        both = jnp.einsum("ned,egdf->gnef", flat, w_gate_up, preferred_element_type=jnp.float32)
        hidden = (jax.nn.silu(both[0]) * both[1]).astype(jnp.bfloat16)
        down = jnp.einsum("nef,efd->ned", hidden, w_down, preferred_element_type=jnp.float32)
        return down.astype(jnp.bfloat16).reshape(groups, capacity, experts_here, model_width)

    arrived = {0: picked_own}
    for step in range(1, req_total):
        if step == 3:
            arrived[step] = partner_move(arrived[1], 2)
        else:
            arrived[step] = partner_move(picked_own, step)
    plan = [[0], [1, 2]] + ([list(range(3, req_total))] if req_total > 3 else [])
    plan = [[k for k in group if k < req_total] for group in plan]
    returned = []
    previous = None
    for group in plan:
        if not group:
            continue
        inputs = [arrived[k] for k in group]
        if previous is not None:
            inputs, previous = lax.optimization_barrier((inputs, previous))
        outs = experts_on(jnp.stack(inputs, axis=0))
        previous = outs
        for slot_index, step in enumerate(group):
            part = outs[slot_index]
            returned.append(part if step == 0 else partner_move(part, step))
    token_weights = jnp.sum(own_combine, axis=-1)
    dispatch_bf = own_dispatch.astype(jnp.bfloat16)
    selected = sum(
        jnp.einsum("tec,ced->ted", dispatch_bf, part, preferred_element_type=jnp.float32)
        for part in returned
    )
    moe_out = jnp.sum(token_weights[:, :, None] * selected, axis=1)
    summed = lax.psum_scatter(
        moe_out.astype(jnp.bfloat16), "head", scatter_dimension=0, tiled=True
    ).astype(jnp.float32)
    rows_out = summed.shape[0]
    kept_rows = lax.dynamic_slice_in_dim(residual, head_index * rows_out, rows_out, 0)
    layer_out = (
        (kept_rows.astype(jnp.float32) + summed)
        .astype(jnp.bfloat16)
        .reshape(1, 1, rows_out, model_width)
    )
    page_pool = pages_in(outgoing, block_owner, block_slot)
    return (layer_out, page_pool)


def solution(mesh):
    return jax.shard_map(
        body,
        mesh=mesh,
        in_specs=(
            P("req", "dev", None),
            P(),
            P(None, None, "head"),
            P("head", None),
            P(),
            P(None, "dev", None),
            P(None, "dev", None),
            P("head", None, None, "req"),
            P("head", "req", None),
            P("req", None, "dev", None, "head"),
            P(),
            P(),
            P(),
        ),
        out_specs=(P("req", "dev", "head", None), P("req", "dev", None, "head")),
        check_vma=False,
    )
```

```python
import jax
import jax.numpy as jnp
from jax import lax
from jax.sharding import PartitionSpec as P

EXPERTS = 8
HD = 64


def shifted(block, axis, distance):
    devices = range(lax.axis_size(axis))
    route = [(i - distance, i) for i in devices if i - distance in devices]
    return lax.ppermute(block, axis, route)


def norm_rows(values, gain_vec):
    widened = values.astype(jnp.float32)
    inv_rms = lax.rsqrt(jnp.mean(widened * widened, axis=-1, keepdims=True) + 1e-05)
    return (widened * inv_rms * gain_vec).astype(jnp.bfloat16)


def rotate(values, positions):
    half_dim = values.shape[-1] // 2
    frequency = 10000.0 ** (-jnp.arange(half_dim, dtype=jnp.float32) / half_dim)
    angles = positions[:, None] * frequency[None, :]
    cosine = jnp.cos(angles)[:, None, :]
    sine_part = jnp.sin(angles)[:, None, :]
    front_half = values[..., :half_dim]
    back_half = values[..., half_dim:]
    return jnp.concatenate(
        [front_half * cosine - back_half * sine_part, back_half * cosine + front_half * sine_part],
        axis=-1,
    )


def slot_tables(route_ids, weights, first_expert, experts_here, capacity):
    expert_ids = first_expert + jnp.arange(experts_here, dtype=jnp.int32)
    matches = (route_ids[..., None] == expert_ids).astype(jnp.float32)
    hit_shape = matches.shape
    flat_hits = matches.reshape(hit_shape[:-3] + (hit_shape[-3] * hit_shape[-2], hit_shape[-1]))
    ranking = (jnp.cumsum(flat_hits, axis=-2) - flat_hits).reshape(hit_shape)
    places = (ranking[..., None] == jnp.arange(capacity, dtype=jnp.float32)).astype(
        jnp.float32
    ) * matches[..., None]
    dispatch = jnp.sum(places, axis=-3)
    combine = jnp.sum(places * weights[..., None, None], axis=-3)
    return (dispatch, combine)


def pages_out(kv_cache, lengths, block_owner, block_slot):
    dev_index = lax.axis_index("dev")
    req_index = lax.axis_index("req")
    owners_total = lax.axis_size("req")
    block_total = block_owner.shape[1]
    finished_total = block_owner.shape[0]
    per_owner = block_total // owners_total
    block_ids = jnp.arange(block_total, dtype=jnp.int32)
    same_owner = block_owner[:, :, None] == block_owner[:, None, :]
    before_mask = block_ids[None, :] < block_ids[:, None]
    page_rank = jnp.sum((same_owner & before_mask[None]).astype(jnp.int32), axis=2)
    own_owner = lax.dynamic_index_in_dim(block_owner, req_index, 0, keepdims=False)
    own_rank = lax.dynamic_index_in_dim(page_rank, req_index, 0, keepdims=False)
    dest_place = own_owner * per_owner + own_rank
    source_block = jnp.sum(
        jnp.where(dest_place[None, :] == block_ids[:, None], block_ids[None, :], 0), axis=1
    )
    page_half = kv_cache.shape[2]
    page_size = page_half * lax.axis_size("dev")
    token_pos = (
        block_ids[:, None] * page_size
        + dev_index * page_half
        + jnp.arange(page_half, dtype=jnp.int32)[None, :]
    )
    own_length = lax.dynamic_index_in_dim(lengths, req_index, 0, keepdims=False)
    live_cache = jnp.where(
        (token_pos < own_length)[:, :, None, None], kv_cache[0], jnp.zeros((), jnp.bfloat16)
    )
    outgoing = jnp.take(live_cache, source_block, axis=0, mode="clip")
    return outgoing


def pages_in(outgoing, block_owner, block_slot):
    req_index = lax.axis_index("req")
    block_total = block_owner.shape[1]
    finished_total = block_owner.shape[0]
    per_owner = block_total // lax.axis_size("req")
    block_ids = jnp.arange(block_total, dtype=jnp.int32)
    same_owner = block_owner[:, :, None] == block_owner[:, None, :]
    before_mask = block_ids[None, :] < block_ids[:, None]
    page_rank = jnp.sum((same_owner & before_mask[None]).astype(jnp.int32), axis=2)
    received = lax.all_to_all(outgoing, "req", split_axis=0, concat_axis=0, tiled=True)
    request_ids = jnp.arange(finished_total, dtype=jnp.int32)
    arrive_place = request_ids[:, None] * per_owner + page_rank
    own_blocks = block_owner == req_index
    slot_match = own_blocks[None] & (block_slot[None] == block_ids[:, None, None])
    gather_place = jnp.sum(jnp.where(slot_match, arrive_place[None], 0), axis=(1, 2))
    page_pool = jnp.take(received, gather_place, axis=0, mode="clip")
    return page_pool


def body(
    tokens,
    attn_gain,
    w_qkv,
    w_out,
    moe_gain,
    routes,
    route_weight,
    w_gate_up,
    w_down,
    kv_cache,
    lengths,
    block_owner,
    block_slot,
):
    half_rows = tokens.shape[1]
    model_width = tokens.shape[2]
    dev_index = lax.axis_index("dev")
    req_index = lax.axis_index("req")
    head_index = lax.axis_index("head")
    local_cols = w_qkv.shape[2]
    head_count = local_cols // HD
    normed = norm_rows(tokens[0], attn_gain)
    projected = jnp.dot(
        normed, w_qkv.reshape(model_width, 3 * local_cols), preferred_element_type=jnp.float32
    ).reshape(half_rows, 3, head_count, HD)
    query_pos = dev_index * half_rows + jnp.arange(half_rows, dtype=jnp.int32)
    angles_at = query_pos.astype(jnp.float32)
    queries = rotate(projected[:, 0], angles_at).astype(jnp.bfloat16)
    key_rows = rotate(projected[:, 1], angles_at).astype(jnp.bfloat16)
    values = projected[:, 2].astype(jnp.bfloat16)
    earlier_both = shifted(jnp.stack([key_rows, values], axis=0), "dev", 1)
    earlier_keys, earlier_values = earlier_both[0], earlier_both[1]
    all_keys = jnp.concatenate([earlier_keys, key_rows], axis=0)
    all_values = jnp.concatenate([earlier_values, values], axis=0)
    key_pos = (dev_index - 1) * half_rows + jnp.arange(2 * half_rows, dtype=jnp.int32)
    allowed = (key_pos[None, :] <= query_pos[:, None]) & (key_pos[None, :] >= 0)
    scores = (
        jnp.einsum("qhd,khd->hqk", queries, all_keys, preferred_element_type=jnp.float32) * 0.125
    )
    scores = jnp.where(allowed[None], scores, -1e30)
    row_peak = jnp.max(scores, axis=-1, keepdims=True)
    exp_scores = jnp.exp(scores - row_peak)
    row_total = jnp.sum(exp_scores, axis=-1)
    attended = (
        jnp.einsum(
            "hqk,khd->qhd",
            exp_scores.astype(jnp.bfloat16),
            all_values,
            preferred_element_type=jnp.float32,
        )
        / jnp.transpose(row_total)[:, :, None]
    )
    attended = attended.astype(jnp.bfloat16).reshape(half_rows, local_cols)
    partial_value = jnp.dot(attended, w_out, preferred_element_type=jnp.float32)
    attn_mixed = lax.psum(partial_value.astype(jnp.bfloat16), "head").astype(jnp.float32)
    residual = (tokens[0].astype(jnp.float32) + attn_mixed).astype(jnp.bfloat16)
    moe_in = norm_rows(residual, moe_gain)
    outgoing = pages_out(kv_cache, lengths, block_owner, block_slot)
    moe_in, outgoing = lax.optimization_barrier((moe_in, outgoing))
    experts_here = w_gate_up.shape[0]
    first_expert = head_index * experts_here
    top_count = routes.shape[2]
    capacity = half_rows * top_count * 3 // (2 * EXPERTS)
    own_routes = lax.dynamic_index_in_dim(routes, req_index, 0, keepdims=True)
    own_weights = lax.dynamic_index_in_dim(route_weight, req_index, 0, keepdims=True)
    own_dispatch, own_combine = slot_tables(
        own_routes, own_weights, first_expert, experts_here, capacity
    )
    own_dispatch = own_dispatch[0]
    own_combine = own_combine[0]
    picked_own = jnp.einsum(
        "tec,td->ced",
        own_dispatch.astype(jnp.bfloat16),
        moe_in,
        preferred_element_type=jnp.float32,
    ).astype(jnp.bfloat16)
    req_total = lax.axis_size("req")

    def partner_move(block, step):
        return lax.ppermute(block, "req", [(i, i ^ step) for i in range(req_total)])

    def experts_on(rows):
        groups = rows.shape[0]
        flat = rows.reshape(groups * capacity, experts_here, model_width)
        both = jnp.einsum("ned,egdf->gnef", flat, w_gate_up, preferred_element_type=jnp.float32)
        hidden = (jax.nn.silu(both[0]) * both[1]).astype(jnp.bfloat16)
        down = jnp.einsum("nef,efd->ned", hidden, w_down, preferred_element_type=jnp.float32)
        return down.astype(jnp.bfloat16).reshape(groups, capacity, experts_here, model_width)

    arrived = {0: picked_own}
    for step in range(1, req_total):
        if step == 3:
            arrived[step] = partner_move(arrived[2], 1)
        else:
            arrived[step] = partner_move(picked_own, step)
    plan = [[0], [1, 2]] + ([list(range(3, req_total))] if req_total > 3 else [])
    plan = [[k for k in group if k < req_total] for group in plan]
    returned = []
    for group in plan:
        if not group:
            continue
        outs = experts_on(jnp.stack([arrived[k] for k in group], axis=0))
        for slot_index, step in enumerate(group):
            part = outs[slot_index]
            returned.append(part if step == 0 else partner_move(part, step))
    token_weights = jnp.sum(own_combine, axis=-1)
    dispatch_bf = own_dispatch.astype(jnp.bfloat16)
    selected = sum(
        jnp.einsum("tec,ced->ted", dispatch_bf, part, preferred_element_type=jnp.float32)
        for part in returned
    )
    moe_out = jnp.sum(token_weights[:, :, None] * selected, axis=1)
    summed = lax.psum_scatter(
        moe_out.astype(jnp.bfloat16), "head", scatter_dimension=0, tiled=True
    ).astype(jnp.float32)
    rows_out = summed.shape[0]
    kept_rows = lax.dynamic_slice_in_dim(residual, head_index * rows_out, rows_out, 0)
    layer_out = (
        (kept_rows.astype(jnp.float32) + summed)
        .astype(jnp.bfloat16)
        .reshape(1, 1, rows_out, model_width)
    )
    page_pool = pages_in(outgoing, block_owner, block_slot)
    return (layer_out, page_pool)


def solution(mesh):
    return jax.shard_map(
        body,
        mesh=mesh,
        in_specs=(
            P("req", "dev", None),
            P(),
            P(None, None, "head"),
            P("head", None),
            P(),
            P(None, "dev", None),
            P(None, "dev", None),
            P("head", None, None, "req"),
            P("head", "req", None),
            P("req", None, "dev", None, "head"),
            P(),
            P(),
            P(),
        ),
        out_specs=(P("req", "dev", "head", None), P("req", "dev", None, "head")),
        check_vma=False,
    )
```
